512 devices in a mesh: dp: 16 (over y, x_lo), table: 32 (over z, x_hi, core).
Axes of the slice: x: 4 (x_hi: 2, x_lo: 2; x = x_hi * 2 + x_lo), y: 8, z: 8, core: 2. Of those that a mesh axis runs over, the one named last changes fastest.
Arguments:
- id_table: bfloat16 [32768, 256], P('table'), may hold values from -2 to 2
- lookup_ids: int32 [65536, 8, 2], P(('dp', 'table')), may hold values from 0 to 32767, as said below
- row_owner: int32 [32768], replicated, may hold values from 0 to 32767, as said below
- query_tower: bfloat16 [1024, 256], replicated, may hold values from -1 to 1
- item_tower: bfloat16 [1024, 256], replicated, may hold values from -1 to 1
- row_seeds: int32 [32768], P('table'), may hold values from 0 to 1073741823
- tower_seeds: int32 [2, 1024], replicated, may hold values from 0 to 1073741823
Outputs:
- table_update: float32 [32768, 256], P('table')
- tower_update: float32 [2, 1024, 256], replicated
The draws below stay inside these ranges and needn't reach their ends.
Inputs may be any that keep to these rules, and one draw needn't show every extreme that they name: `lookup_ids`: in every aligned block of 128 examples (the examples of one device), at most 96 of the lookups have row_owner[id] // 1024 equal to any one table shard, and exactly 96 do for some shard. A permutation: the row of id i lies at position row_owner[i] of id_table, on table shard row_owner[i] // 1024.
All inputs are finite; a program needn't handle non-finite values.
Results may differ from the reference program's by a relative error of at most 0.0073.
The reference program's roundings to bfloat16 on the way (of `pooled`, `probs`, `query_grad`, `item_grad` and `lookup_grad`) count: a program that leaves them out, or rounds other values in their place, can miss the bound.
Values may be sent and summed in bfloat16 or wider, within the bound.
No kernel may reach another device: no remote copies, remote signals or barrier semaphores. Data moves between devices by JAX's collectives and lax.ppermute only.
A program may use at most 64 MiB of HBM per device.

```python
import math
import jax
import jax.numpy as jnp
from jax import lax

EMB = 256
FEAT = 4
BAG = 2
OUT = 256
ROWS_DEV = 1024
B_DEV = 128
HID = 1024
VOCAB = 32768
EXAMPLES = 65536
N_DP = 16
N_TABLE = 32


def owner_order(key):
    return jax.random.permutation(jax.random.fold_in(key, 11), VOCAB).astype(jnp.int32)


def draw_row_owner(key, part):
    return owner_order(key)


def shard_order(shard_key):
    return jax.random.permutation(shard_key, ROWS_DEV).astype(jnp.int32)


def draw_lookup_ids(key, part):
    placed = owner_order(key)
    inverse = jnp.argsort(placed).astype(jnp.int32)
    shards = VOCAB // ROWS_DEV
    half = B_DEV * FEAT * BAG
    half_cap = 3 * half // (2 * shards)
    blocks = EXAMPLES // B_DEV
    heavy = jax.random.randint(jax.random.fold_in(key, 12), (), 0, shards).astype(jnp.int32)
    others = jnp.arange(shards - 1, dtype=jnp.int32)
    others = others + (others >= heavy).astype(jnp.int32)
    spare = jnp.repeat(others, half_cap)
    used_count = jax.random.randint(jax.random.fold_in(key, 14), (shards,), ROWS_DEV // 2, 7 * ROWS_DEV // 8 + 1).astype(jnp.int32)
    shard_keys = jax.random.split(jax.random.fold_in(key, 15), shards)
    used_rows = jax.vmap(shard_order)(shard_keys)

    def choose_rows(owner_ids, draw_key):
        drawn = jax.random.randint(draw_key, owner_ids.shape, 0, 1048576).astype(jnp.int32)
        return used_rows[owner_ids, drawn % used_count[owner_ids]]

    def one_block(block_key):
        subkeys = jax.random.split(block_key, 6)
        chosen = jax.random.permutation(subkeys[0], spare)[:half - half_cap]
        query_owner = jax.random.permutation(subkeys[1], jnp.concatenate([jnp.full((half_cap,), heavy, jnp.int32), chosen]))
        query_owner = query_owner.reshape(B_DEV, FEAT * BAG)
        query_local = choose_rows(query_owner, subkeys[2])
        shuffle = jax.random.permutation(subkeys[3], B_DEV)
        aligned = jax.random.randint(subkeys[4], (B_DEV, 1), 0, 4) == 0
        item_owner = query_owner[shuffle]
        fresh = choose_rows(item_owner, subkeys[5])
        item_local = jnp.where(aligned, query_local[shuffle], fresh)
        spots = jnp.concatenate([query_owner * ROWS_DEV + query_local, item_owner * ROWS_DEV + item_local], axis=1)
        return inverse[spots].reshape(B_DEV, 2 * FEAT, BAG)
    block_keys = jax.random.split(jax.random.fold_in(key, 13), blocks)
    return jax.vmap(one_block)(block_keys).reshape(EXAMPLES, 2 * FEAT, BAG).astype(jnp.int32)


def draw_id_table(key, part):
    values = jax.random.normal(jax.random.fold_in(key, 3), (VOCAB, EMB), jnp.float32)
    values = 0.05 * values
    return jnp.clip(values, -2.0, 2.0).astype(jnp.bfloat16)


def tower_pair(key):
    first = jax.random.normal(jax.random.fold_in(key, 21), (HID, OUT), jnp.float32) / math.sqrt(HID)
    second = jax.random.normal(jax.random.fold_in(key, 22), (HID, OUT), jnp.float32) / math.sqrt(HID)
    return (jnp.clip(first, -1.0, 1.0), jnp.clip(second, -1.0, 1.0))


def draw_query_tower(key, part):
    return tower_pair(key)[0].astype(jnp.bfloat16)


def draw_item_tower(key, part):
    return tower_pair(key)[1].astype(jnp.bfloat16)


def touch_ends(array, own_key, low, top_value):
    extent = array.shape
    index_at = [jax.random.randint(jax.random.fold_in(own_key, axis), (), 0, extent[axis]) for axis in range(len(extent))]
    array = array.at[tuple(index_at)].set(low)
    longest = extent.index(max(extent))
    index_at[longest] = (index_at[longest] + 1) % extent[longest]
    return array.at[tuple(index_at)].set(top_value)


def setup_inputs(seed: int = 0) -> dict:
    keys = jax.random.split(jax.random.key(seed), 8)
    return {
        "id_table": draw_id_table(jax.random.fold_in(keys[7], 71), 0),
        "lookup_ids": draw_lookup_ids(jax.random.fold_in(keys[7], 71), 0),
        "row_owner": draw_row_owner(jax.random.fold_in(keys[7], 71), 0),
        "query_tower": draw_query_tower(jax.random.fold_in(keys[7], 71), 0),
        "item_tower": draw_item_tower(jax.random.fold_in(keys[7], 71), 0),
        "row_seeds": touch_ends(jax.random.randint(keys[5], (VOCAB,), 0, 1073741824), jax.random.fold_in(keys[5], 1), 0, 1073741823).astype(jnp.int32),
        "tower_seeds": touch_ends(jax.random.randint(keys[6], (2, HID), 0, 1073741824), jax.random.fold_in(keys[6], 1), 0, 1073741823).astype(jnp.int32),
    }


NOISE_MULT = 0.1

def hashed_noise(seed_rows, width):
    columns = jnp.arange(width, dtype=jnp.int32)
    summed = jnp.zeros(seed_rows.shape + (width,), jnp.float32)
    for section in range(2):
        mixed = seed_rows[..., None] + (columns * 2 + section) * 1013904223
        mixed = mixed ^ mixed >> 15 & 131071
        mixed = mixed * 73244475
        mixed = mixed ^ mixed >> 13 & 524287
        mixed = mixed * 1597334677
        mixed = mixed ^ mixed >> 16 & 65535
        lower = (mixed & 65535).astype(jnp.float32) / 65536.0 - 0.5
        upper = (mixed >> 16 & 65535).astype(jnp.float32) / 65536.0 - 0.5
        summed = summed + lower + upper
    return summed * math.sqrt(3.0)

def squares(values):
    return lax.optimization_barrier(jnp.sum(jnp.square(values.astype(jnp.float32)), axis=1))

def reference(id_table, lookup_ids, row_owner, query_tower, item_tower, row_seeds, tower_seeds):
    scale = 200.0 / math.sqrt(OUT)
    clip_norm = 0.9 * math.sqrt(2.0 * HID + 400.0)
    slots = 2 * FEAT
    group_rows = N_DP * B_DEV
    positions = row_owner[lookup_ids]
    grouped = positions.reshape(N_DP, N_TABLE, B_DEV, slots, BAG).transpose(1, 0, 2, 3, 4)
    grouped = grouped.reshape(N_TABLE, group_rows, slots, BAG)

    def one_group(carry, group_pos):
        tower_sum, row_sum, row_count = carry
        looked = id_table[group_pos]
        pooled = lax.optimization_barrier(jnp.sum(looked.astype(jnp.float32), axis=2)).astype(jnp.bfloat16)
        query_in = pooled[:, :FEAT].reshape(group_rows, HID)
        item_in = pooled[:, FEAT:].reshape(group_rows, HID)
        query_vec = jnp.dot(query_in, query_tower, preferred_element_type=jnp.float32).astype(jnp.bfloat16)
        item_vec = jnp.dot(item_in, item_tower, preferred_element_type=jnp.float32).astype(jnp.bfloat16)
        scores = scale * jnp.dot(query_vec, item_vec.T, preferred_element_type=jnp.float32)
        peak = lax.optimization_barrier(jnp.max(scores, axis=1, keepdims=True))
        log_total = peak + jnp.log(lax.optimization_barrier(jnp.sum(jnp.exp(scores - peak), axis=1, keepdims=True)))
        probs = jnp.exp(scores - log_total).astype(jnp.bfloat16)
        query_grad = (scale * (jnp.dot(probs, item_vec, preferred_element_type=jnp.float32) - item_vec.astype(jnp.float32))).astype(jnp.bfloat16)
        item_grad = (scale * (jnp.dot(probs.T, query_vec, preferred_element_type=jnp.float32) - query_vec.astype(jnp.float32))).astype(jnp.bfloat16)
        query_back = jnp.dot(query_grad, query_tower.T, preferred_element_type=jnp.float32)
        item_back = jnp.dot(item_grad, item_tower.T, preferred_element_type=jnp.float32)
        norm_sq = squares(query_in) * squares(query_grad) + squares(item_in) * squares(item_grad) + squares(query_back) + squares(item_back)
        factor = jnp.minimum(1.0, clip_norm / jnp.sqrt(norm_sq + 1e-06))
        clipped_query = (factor[:, None] * query_grad.astype(jnp.float32)).astype(jnp.bfloat16)
        clipped_item = (factor[:, None] * item_grad.astype(jnp.float32)).astype(jnp.bfloat16)
        tower_step = jnp.stack([jnp.dot(query_in.T, clipped_query, preferred_element_type=jnp.float32), jnp.dot(item_in.T, clipped_item, preferred_element_type=jnp.float32)])
        back_all = jnp.concatenate([query_back.reshape(group_rows, FEAT, EMB), item_back.reshape(group_rows, FEAT, EMB)], axis=1)
        lookup_grad = (factor[:, None, None] * back_all).astype(jnp.bfloat16)
        spread = jnp.broadcast_to(lookup_grad[:, :, None, :], (group_rows, slots, BAG, EMB))
        spread = spread.reshape(group_rows * slots * BAG, EMB).astype(jnp.float32)
        flat_pos = group_pos.reshape(-1)
        row_sum = row_sum.at[flat_pos].add(spread)
        row_count = row_count.at[flat_pos].add(jnp.ones(flat_pos.shape, jnp.float32))
        return ((tower_sum + tower_step, row_sum, row_count), None)
    start = (jnp.zeros((2, HID, OUT), jnp.float32), jnp.zeros((VOCAB, EMB), jnp.float32), jnp.zeros((VOCAB,), jnp.float32))
    (tower_sum, row_sum, row_count), unused = lax.scan(one_group, start, grouped)
    row_noise = hashed_noise(row_seeds, EMB)
    table_update = row_sum / clip_norm + NOISE_MULT * jnp.where(row_count[:, None] > 0.0, row_noise, 0.0)
    tower_update = tower_sum / clip_norm + NOISE_MULT * hashed_noise(tower_seeds, OUT)
    return (table_update, tower_update)
```

```python
import math

import jax
import jax.numpy as jnp
from jax import lax
from jax.sharding import PartitionSpec as P

NOISE_MULT = 0.1


def hashed_noise(seed_rows, width):
    columns = jnp.arange(width, dtype=jnp.int32)
    summed = jnp.zeros(seed_rows.shape + (width,), jnp.float32)
    for section in range(2):
        mixed = seed_rows[..., None] + (columns * 2 + section) * 1013904223
        mixed = mixed ^ mixed >> 15 & 131071
        mixed = mixed * 73244475
        mixed = mixed ^ mixed >> 13 & 524287
        mixed = mixed * 1597334677
        mixed = mixed ^ mixed >> 16 & 65535
        lower = (mixed & 65535).astype(jnp.float32) / 65536.0 - 0.5
        upper = (mixed >> 16 & 65535).astype(jnp.float32) / 65536.0 - 0.5
        summed = summed + lower + upper
    return summed * math.sqrt(3.0)


def squares(values):
    return jnp.sum(jnp.square(values.astype(jnp.float32)), axis=1)


def body(id_table, lookup_ids, row_owner, query_tower, item_tower, row_seeds, tower_seeds):
    shards = lax.axis_size("table")
    rows_dev, emb_width = id_table.shape
    batch, slots, bags = lookup_ids.shape
    feats = slots // 2
    hidden_width, out_width = query_tower.shape
    scale = 200.0 / math.sqrt(out_width)
    clip_norm = 0.9 * math.sqrt(2.0 * hidden_width + 400.0)
    requests = batch * slots * bags
    capacity = 3 * requests // (2 * shards)
    positions = row_owner[lookup_ids.reshape(-1)]
    owners = positions // rows_dev
    local_rows = positions - owners * rows_dev
    one_hot = (owners[:, None] == jnp.arange(shards, dtype=jnp.int32)[None, :]).astype(jnp.int32)
    ranks = jnp.sum((jnp.cumsum(one_hot, axis=0) - one_hot) * one_hot, axis=1)
    targets = owners * capacity + ranks
    outgoing = jnp.full((shards * capacity,), -1, jnp.int32).at[targets].set(local_rows)
    outgoing = outgoing.reshape(shards, capacity)
    incoming = lax.all_to_all(outgoing, "table", split_axis=0, concat_axis=0, tiled=True)
    valid = incoming >= 0
    fetched = id_table[jnp.where(valid, incoming, 0)]
    fetched = jnp.where(valid[:, :, None], fetched, jnp.zeros((), jnp.bfloat16))
    returned = lax.all_to_all(fetched, "table", split_axis=0, concat_axis=0, tiled=True)
    returned, incoming = (returned, incoming)
    looked = returned.reshape(shards * capacity, emb_width)[targets]
    pooled = jnp.sum(looked.reshape(batch, slots, bags, emb_width).astype(jnp.float32), axis=2)
    pooled = pooled.astype(jnp.bfloat16)
    query_in = pooled[:, :feats].reshape(batch, hidden_width)
    item_in = pooled[:, feats:].reshape(batch, hidden_width)
    query_vec = jnp.dot(query_in, query_tower, preferred_element_type=jnp.float32).astype(
        jnp.bfloat16
    )
    item_vec = jnp.dot(item_in, item_tower, preferred_element_type=jnp.float32).astype(jnp.bfloat16)
    n_dp = lax.axis_size("dp")
    dp_index = lax.axis_index("dp")
    table_index = lax.axis_index("table")
    both = jnp.concatenate([query_vec, item_vec], axis=1)
    both = lax.all_to_all(
        jnp.broadcast_to(both[None], (n_dp,) + both.shape), "dp", 0, 0, tiled=True
    )
    all_queries = both[:, :, :out_width].reshape(n_dp * batch, out_width)
    all_items = both[:, :, out_width:].reshape(n_dp * batch, out_width)
    scores = scale * lax.dot_general(
        all_queries, all_items, (((1,), (1,)), ((), ())), preferred_element_type=jnp.float32
    )
    peak = jnp.max(scores, axis=1, keepdims=True)
    log_total = peak + jnp.log(jnp.sum(jnp.exp(scores - peak), axis=1, keepdims=True))
    own = dp_index * batch
    row_scores = lax.dynamic_slice_in_dim(scores, own, batch, axis=0)
    row_total = lax.dynamic_slice_in_dim(log_total, own, batch, axis=0)
    col_scores = lax.dynamic_slice_in_dim(scores, own, batch, axis=1)
    row_probs = jnp.exp(row_scores - row_total).astype(jnp.bfloat16)
    col_probs = jnp.exp(col_scores - log_total).astype(jnp.bfloat16)
    query_grad = (
        scale
        * (
            jnp.dot(row_probs, all_items, preferred_element_type=jnp.float32)
            - item_vec.astype(jnp.float32)
        )
    ).astype(jnp.bfloat16)
    weighted = lax.dot_general(
        col_probs, all_queries, (((0,), (0,)), ((), ())), preferred_element_type=jnp.float32
    )
    item_grad = (scale * (weighted - query_vec.astype(jnp.float32))).astype(jnp.bfloat16)
    query_back = lax.dot_general(
        query_grad, query_tower, (((1,), (1,)), ((), ())), preferred_element_type=jnp.float32
    )
    item_back = lax.dot_general(
        item_grad, item_tower, (((1,), (1,)), ((), ())), preferred_element_type=jnp.float32
    )
    norm_sq = (
        squares(query_in) * squares(query_grad)
        + squares(item_in) * squares(item_grad)
        + squares(query_back)
        + squares(item_back)
    )
    factor = jnp.minimum(1.0, clip_norm / jnp.sqrt(norm_sq + 1e-06))
    clipped_query = (factor[:, None] * query_grad.astype(jnp.float32)).astype(jnp.bfloat16)
    clipped_item = (factor[:, None] * item_grad.astype(jnp.float32)).astype(jnp.bfloat16)
    tower_part = jnp.stack(
        [
            lax.dot_general(
                query_in,
                clipped_query,
                (((0,), (0,)), ((), ())),
                preferred_element_type=jnp.float32,
            ),
            lax.dot_general(
                item_in, clipped_item, (((0,), (0,)), ((), ())), preferred_element_type=jnp.float32
            ),
        ]
    )
    back_all = jnp.concatenate(
        [query_back.reshape(batch, feats, emb_width), item_back.reshape(batch, feats, emb_width)],
        axis=1,
    )
    lookup_grad = (factor[:, None, None] * back_all).astype(jnp.bfloat16)
    spread = jnp.broadcast_to(lookup_grad[:, :, None, :], (batch, slots, bags, emb_width))
    spread = spread.reshape(requests, emb_width)
    grad_out = jnp.zeros((shards * capacity, emb_width), jnp.bfloat16).at[targets].set(spread)
    grad_in = lax.all_to_all(
        grad_out.reshape(shards, capacity, emb_width),
        "table",
        split_axis=0,
        concat_axis=0,
        tiled=True,
    )
    flat_in = incoming.reshape(-1)
    slot_rows = jnp.where(flat_in >= 0, flat_in, rows_dev)
    row_sum = (
        jnp.zeros((rows_dev, emb_width), jnp.float32)
        .at[slot_rows]
        .add(grad_in.reshape(shards * capacity, emb_width).astype(jnp.float32), mode="drop")
    )
    row_count = (
        jnp.zeros((rows_dev,), jnp.float32)
        .at[slot_rows]
        .add((flat_in >= 0).astype(jnp.float32), mode="drop")
    )
    shard_rows = rows_dev // n_dp
    packed = jnp.concatenate(
        [
            row_sum.reshape(n_dp, shard_rows, emb_width),
            jnp.broadcast_to(row_count.reshape(n_dp, 1, shard_rows, 1), (n_dp, 1, shard_rows, emb_width // shard_rows))
            .reshape(n_dp, 1, emb_width),
        ],
        axis=1,
    )
    packed = jnp.sum(lax.all_to_all(packed, "dp", 0, 0, tiled=True), axis=0)
    own_sum = packed[:shard_rows]
    own_count = packed[shard_rows].reshape(shard_rows, emb_width // shard_rows)[:, 0]
    own_seeds = lax.dynamic_slice_in_dim(row_seeds, dp_index * shard_rows, shard_rows)
    own_update = own_sum / clip_norm + NOISE_MULT * jnp.where(
        own_count[:, None] > 0.0, hashed_noise(own_seeds, emb_width), 0.0
    )
    table_update = lax.all_to_all(
        jnp.broadcast_to(own_update[None], (n_dp,) + own_update.shape), "dp", 0, 0, tiled=True
    ).reshape(rows_dev, emb_width)
    tower_rows = 2 * hidden_width
    dp_rows = tower_rows // n_dp
    part = tower_part.reshape(n_dp, dp_rows, out_width)
    part = jnp.sum(lax.all_to_all(part, "dp", 0, 0, tiled=True), axis=0)
    own_rows = dp_rows // shards
    part = part.reshape(shards, own_rows, out_width)
    part = jnp.sum(lax.all_to_all(part, "table", 0, 0, tiled=True), axis=0)
    first_row = dp_index * dp_rows + table_index * own_rows
    tower_seed_rows = lax.dynamic_slice_in_dim(tower_seeds.reshape(tower_rows), first_row, own_rows)
    part = part / clip_norm + NOISE_MULT * hashed_noise(tower_seed_rows, out_width)
    part = lax.all_to_all(
        jnp.broadcast_to(part[None], (shards,) + part.shape), "table", 0, 0, tiled=True
    ).reshape(dp_rows, out_width)
    tower_update = lax.all_to_all(
        jnp.broadcast_to(part[None], (n_dp,) + part.shape), "dp", 0, 0, tiled=True
    ).reshape(2, hidden_width, out_width)
    return (table_update, tower_update)


def solution(mesh):
    in_specs = (P("table", None), P(("dp", "table"), None, None), P(), P(), P(), P("table"), P())
    out_specs = (P("table", None), P())
    return jax.shard_map(body, mesh=mesh, in_specs=in_specs, out_specs=out_specs, check_vma=False)
```

```python
import math

import jax
import jax.numpy as jnp
from jax import lax
from jax.sharding import PartitionSpec as P

NOISE_MULT = 0.1


def hashed_noise(seed_rows, width):
    columns = jnp.arange(width, dtype=jnp.int32)
    summed = jnp.zeros(seed_rows.shape + (width,), jnp.float32)
    for section in range(2):
        mixed = seed_rows[..., None] + (columns * 2 + section) * 1013904223
        mixed = mixed ^ mixed >> 15 & 131071
        mixed = mixed * 73244475
        mixed = mixed ^ mixed >> 13 & 524287
        mixed = mixed * 1597334677
        mixed = mixed ^ mixed >> 16 & 65535
        lower = (mixed & 65535).astype(jnp.float32) / 65536.0 - 0.5
        upper = (mixed >> 16 & 65535).astype(jnp.float32) / 65536.0 - 0.5
        summed = summed + lower + upper
    return summed * math.sqrt(3.0)


def squares(values):
    return jnp.sum(jnp.square(values.astype(jnp.float32)), axis=1)


def body(id_table, lookup_ids, row_owner, query_tower, item_tower, row_seeds, tower_seeds):
    shards = lax.axis_size("table")
    rows_dev, emb_width = id_table.shape
    batch, slots, bags = lookup_ids.shape
    feats = slots // 2
    hidden_width, out_width = query_tower.shape
    scale = 200.0 / math.sqrt(out_width)
    clip_norm = 0.9 * math.sqrt(2.0 * hidden_width + 400.0)
    requests = batch * slots * bags
    capacity = 3 * requests // (2 * shards)
    positions = row_owner[lookup_ids.reshape(-1)]
    owners = positions // rows_dev
    local_rows = positions - owners * rows_dev
    one_hot = owners[:, None] == jnp.arange(shards, dtype=jnp.int32)[None, :]
    order = jnp.arange(requests, dtype=jnp.int32)
    earlier = (order[None, :] < order[:, None]).astype(jnp.bfloat16)
    before = jnp.dot(earlier, one_hot.astype(jnp.bfloat16), preferred_element_type=jnp.float32)
    ranks = jnp.sum(jnp.where(one_hot, before, 0.0), axis=1).astype(jnp.int32)
    targets = owners * capacity + ranks
    slots_all = jnp.arange(shards * capacity, dtype=jnp.int32)
    slot_match = targets[:, None] == slots_all[None, :]
    outgoing = jnp.max(jnp.where(slot_match, local_rows[:, None], -1), axis=0)
    outgoing = outgoing.reshape(shards, capacity)
    incoming = lax.all_to_all(outgoing, "table", split_axis=0, concat_axis=0, tiled=True)
    flat_in = incoming.reshape(-1)
    row_match = (flat_in[:, None] == jnp.arange(rows_dev, dtype=jnp.int32)[None, :]).astype(
        jnp.bfloat16
    )
    fetched = jnp.dot(row_match, id_table, preferred_element_type=jnp.float32).astype(jnp.bfloat16)
    returned = lax.all_to_all(
        fetched.reshape(shards, capacity, emb_width), "table", split_axis=0, concat_axis=0, tiled=True
    )
    pair_targets = targets.reshape(batch * slots, bags)
    pool_match = pair_targets[:, 0:1] == slots_all[None, :]
    for bag in range(1, bags):
        pool_match = pool_match | (pair_targets[:, bag : bag + 1] == slots_all[None, :])
    pool_match = pool_match.astype(jnp.bfloat16)
    pooled = jnp.dot(
        pool_match,
        returned.reshape(shards * capacity, emb_width),
        preferred_element_type=jnp.float32,
    )
    pooled = pooled.astype(jnp.bfloat16).reshape(batch, slots, emb_width)
    query_in = pooled[:, :feats].reshape(batch, hidden_width)
    item_in = pooled[:, feats:].reshape(batch, hidden_width)
    query_vec = jnp.dot(query_in, query_tower, preferred_element_type=jnp.float32).astype(
        jnp.bfloat16
    )
    item_vec = jnp.dot(item_in, item_tower, preferred_element_type=jnp.float32).astype(jnp.bfloat16)
    n_dp = lax.axis_size("dp")
    dp_index = lax.axis_index("dp")
    table_index = lax.axis_index("table")
    both = jnp.concatenate([query_vec, item_vec], axis=1)
    both = lax.all_to_all(
        jnp.broadcast_to(both[None], (n_dp,) + both.shape), "dp", 0, 0, tiled=True
    )
    all_queries = both[:, :, :out_width].reshape(n_dp * batch, out_width)
    all_items = both[:, :, out_width:].reshape(n_dp * batch, out_width)
    scores = scale * lax.dot_general(
        all_queries, all_items, (((1,), (1,)), ((), ())), preferred_element_type=jnp.float32
    )
    peak = jnp.max(scores, axis=1, keepdims=True)
    log_total = peak + jnp.log(jnp.sum(jnp.exp(scores - peak), axis=1, keepdims=True))
    own = dp_index * batch
    row_scores = lax.dynamic_slice_in_dim(scores, own, batch, axis=0)
    row_total = lax.dynamic_slice_in_dim(log_total, own, batch, axis=0)
    col_scores = lax.dynamic_slice_in_dim(scores, own, batch, axis=1)
    row_probs = jnp.exp(row_scores - row_total).astype(jnp.bfloat16)
    col_probs = jnp.exp(col_scores - log_total).astype(jnp.bfloat16)
    query_grad = (
        scale
        * (
            jnp.dot(row_probs, all_items, preferred_element_type=jnp.float32)
            - item_vec.astype(jnp.float32)
        )
    ).astype(jnp.bfloat16)
    weighted = lax.dot_general(
        col_probs, all_queries, (((0,), (0,)), ((), ())), preferred_element_type=jnp.float32
    )
    item_grad = (scale * (weighted - query_vec.astype(jnp.float32))).astype(jnp.bfloat16)
    query_back = lax.dot_general(
        query_grad, query_tower, (((1,), (1,)), ((), ())), preferred_element_type=jnp.float32
    )
    item_back = lax.dot_general(
        item_grad, item_tower, (((1,), (1,)), ((), ())), preferred_element_type=jnp.float32
    )
    norm_sq = (
        squares(query_in) * squares(query_grad)
        + squares(item_in) * squares(item_grad)
        + squares(query_back)
        + squares(item_back)
    )
    factor = jnp.minimum(1.0, clip_norm / jnp.sqrt(norm_sq + 1e-06))
    clipped_query = (factor[:, None] * query_grad.astype(jnp.float32)).astype(jnp.bfloat16)
    clipped_item = (factor[:, None] * item_grad.astype(jnp.float32)).astype(jnp.bfloat16)
    tower_part = jnp.stack(
        [
            lax.dot_general(
                query_in,
                clipped_query,
                (((0,), (0,)), ((), ())),
                preferred_element_type=jnp.float32,
            ),
            lax.dot_general(
                item_in, clipped_item, (((0,), (0,)), ((), ())), preferred_element_type=jnp.float32
            ),
        ]
    )
    back_all = jnp.concatenate(
        [query_back.reshape(batch, feats, emb_width), item_back.reshape(batch, feats, emb_width)],
        axis=1,
    )
    lookup_grad = (factor[:, None, None] * back_all).astype(jnp.bfloat16)
    grad_out = lax.dot_general(
        pool_match,
        lookup_grad.reshape(batch * slots, emb_width),
        (((0,), (0,)), ((), ())),
        preferred_element_type=jnp.float32,
    ).astype(jnp.bfloat16)
    grad_in = lax.all_to_all(
        grad_out.reshape(shards, capacity, emb_width),
        "table",
        split_axis=0,
        concat_axis=0,
        tiled=True,
    )
    row_sum = lax.dot_general(
        row_match,
        grad_in.reshape(shards * capacity, emb_width),
        (((0,), (0,)), ((), ())),
        preferred_element_type=jnp.float32,
    )
    row_count = jnp.sum(row_match.astype(jnp.float32), axis=0)
    shard_rows = rows_dev // n_dp
    packed = jnp.concatenate(
        [
            row_sum.reshape(n_dp, shard_rows, emb_width),
            jnp.broadcast_to(row_count.reshape(n_dp, 1, shard_rows, 1), (n_dp, 1, shard_rows, emb_width // shard_rows))
            .reshape(n_dp, 1, emb_width),
        ],
        axis=1,
    )
    packed = jnp.sum(lax.all_to_all(packed, "dp", 0, 0, tiled=True), axis=0)
    own_sum = packed[:shard_rows]
    own_count = packed[shard_rows].reshape(shard_rows, emb_width // shard_rows)[:, 0]
    own_seeds = lax.dynamic_slice_in_dim(row_seeds, dp_index * shard_rows, shard_rows)
    own_update = own_sum / clip_norm + NOISE_MULT * jnp.where(
        own_count[:, None] > 0.0, hashed_noise(own_seeds, emb_width), 0.0
    )
    table_update = lax.all_to_all(
        jnp.broadcast_to(own_update[None], (n_dp,) + own_update.shape), "dp", 0, 0, tiled=True
    ).reshape(rows_dev, emb_width)
    tower_rows = 2 * hidden_width
    dp_rows = tower_rows // n_dp
    part = tower_part.reshape(n_dp, dp_rows, out_width)
    part = jnp.sum(lax.all_to_all(part, "dp", 0, 0, tiled=True), axis=0)
    own_rows = dp_rows // shards
    part = part.reshape(shards, own_rows, out_width)
    part = jnp.sum(lax.all_to_all(part, "table", 0, 0, tiled=True), axis=0)
    first_row = dp_index * dp_rows + table_index * own_rows
    tower_seed_rows = lax.dynamic_slice_in_dim(tower_seeds.reshape(tower_rows), first_row, own_rows)
    part = part / clip_norm + NOISE_MULT * hashed_noise(tower_seed_rows, out_width)
    part = lax.all_to_all(
        jnp.broadcast_to(part[None], (shards,) + part.shape), "table", 0, 0, tiled=True
    ).reshape(dp_rows, out_width)
    tower_update = lax.all_to_all(
        jnp.broadcast_to(part[None], (n_dp,) + part.shape), "dp", 0, 0, tiled=True
    ).reshape(2, hidden_width, out_width)
    return (table_update, tower_update)


def solution(mesh):
    in_specs = (P("table", None), P(("dp", "table"), None, None), P(), P(), P(), P("table"), P())
    out_specs = (P("table", None), P())
    return jax.shard_map(body, mesh=mesh, in_specs=in_specs, out_specs=out_specs, check_vma=False)
```

```python
import math

import jax
import jax.numpy as jnp
from jax import lax
from jax.sharding import PartitionSpec as P

NOISE_MULT = 0.1


def hashed_noise(seed_rows, width):
    columns = jnp.arange(width, dtype=jnp.int32)
    summed = jnp.zeros(seed_rows.shape + (width,), jnp.float32)
    for section in range(2):
        mixed = seed_rows[..., None] + (columns * 2 + section) * 1013904223
        mixed = mixed ^ mixed >> 15 & 131071
        mixed = mixed * 73244475
        mixed = mixed ^ mixed >> 13 & 524287
        mixed = mixed * 1597334677
        mixed = mixed ^ mixed >> 16 & 65535
        lower = (mixed & 65535).astype(jnp.float32) / 65536.0 - 0.5
        upper = (mixed >> 16 & 65535).astype(jnp.float32) / 65536.0 - 0.5
        summed = summed + lower + upper
    return summed * math.sqrt(3.0)


def squares(values):
    return jnp.sum(jnp.square(values.astype(jnp.float32)), axis=1)


def body(id_table, lookup_ids, row_owner, query_tower, item_tower, row_seeds, tower_seeds):
    shards = lax.axis_size("table")
    rows_dev, emb_width = id_table.shape
    batch, slots, bags = lookup_ids.shape
    feats = slots // 2
    hidden_width, out_width = query_tower.shape
    scale = 200.0 / math.sqrt(out_width)
    clip_norm = 0.9 * math.sqrt(2.0 * hidden_width + 400.0)
    requests = batch * slots * bags
    capacity = 3 * requests // (2 * shards)
    positions = row_owner[lookup_ids.reshape(-1)]
    owners = positions // rows_dev
    local_rows = positions - owners * rows_dev
    one_hot = owners[:, None] == jnp.arange(shards, dtype=jnp.int32)[None, :]
    order = jnp.arange(requests, dtype=jnp.int32)
    earlier = (order[None, :] < order[:, None]).astype(jnp.bfloat16)
    before = jnp.dot(earlier, one_hot.astype(jnp.bfloat16), preferred_element_type=jnp.float32)
    ranks = jnp.sum(jnp.where(one_hot, before, 0.0), axis=1).astype(jnp.int32)
    targets = owners * capacity + ranks
    slots_all = jnp.arange(shards * capacity, dtype=jnp.int32)
    slot_match = targets[:, None] == slots_all[None, :]
    outgoing = jnp.max(jnp.where(slot_match, local_rows[:, None], -1), axis=0)
    outgoing = outgoing.reshape(shards, capacity)
    incoming = lax.all_to_all(outgoing, "table", split_axis=0, concat_axis=0, tiled=True)
    flat_in = incoming.reshape(-1)
    row_match = (flat_in[:, None] == jnp.arange(rows_dev, dtype=jnp.int32)[None, :]).astype(
        jnp.bfloat16
    )
    fetched = jnp.dot(row_match, id_table, preferred_element_type=jnp.float32).astype(jnp.bfloat16)
    returned = lax.all_to_all(
        fetched.reshape(shards, capacity, emb_width), "table", split_axis=0, concat_axis=0, tiled=True
    )
    pair_targets = targets.reshape(batch * slots, bags)
    pool_match = pair_targets[:, 0:1] == slots_all[None, :]
    for bag in range(1, bags):
        pool_match = pool_match | (pair_targets[:, bag : bag + 1] == slots_all[None, :])
    pool_match = pool_match.astype(jnp.bfloat16)
    pooled = jnp.dot(
        pool_match,
        returned.reshape(shards * capacity, emb_width),
        preferred_element_type=jnp.float32,
    )
    pooled = pooled.astype(jnp.bfloat16).reshape(batch, slots, emb_width)
    query_in = pooled[:, :feats].reshape(batch, hidden_width)
    item_in = pooled[:, feats:].reshape(batch, hidden_width)
    query_vec = jnp.dot(query_in, query_tower, preferred_element_type=jnp.float32).astype(
        jnp.bfloat16
    )
    item_vec = jnp.dot(item_in, item_tower, preferred_element_type=jnp.float32).astype(jnp.bfloat16)
    n_dp = lax.axis_size("dp")
    dp_index = lax.axis_index("dp")
    table_index = lax.axis_index("table")
    both = jnp.concatenate([query_vec, item_vec], axis=1)
    both = lax.all_to_all(
        jnp.broadcast_to(both[None], (n_dp,) + both.shape), "dp", 0, 0, tiled=True
    )
    all_queries = both[:, :, :out_width].reshape(n_dp * batch, out_width)
    all_items = both[:, :, out_width:].reshape(n_dp * batch, out_width)
    scores = scale * lax.dot_general(
        all_queries, all_items, (((1,), (1,)), ((), ())), preferred_element_type=jnp.float32
    )
    peak = jnp.max(scores, axis=1, keepdims=True)
    log_total = peak + jnp.log(jnp.sum(jnp.exp(scores - peak), axis=1, keepdims=True))
    own = dp_index * batch
    row_scores = lax.dynamic_slice_in_dim(scores, own, batch, axis=0)
    row_total = lax.dynamic_slice_in_dim(log_total, own, batch, axis=0)
    col_scores = lax.dynamic_slice_in_dim(scores, own, batch, axis=1)
    row_probs = jnp.exp(row_scores - row_total).astype(jnp.bfloat16)
    col_probs = jnp.exp(col_scores - log_total).astype(jnp.bfloat16)
    query_grad = (
        scale
        * (
            jnp.dot(row_probs, all_items, preferred_element_type=jnp.float32)
            - item_vec.astype(jnp.float32)
        )
    ).astype(jnp.bfloat16)
    weighted = lax.dot_general(
        col_probs, all_queries, (((0,), (0,)), ((), ())), preferred_element_type=jnp.float32
    )
    item_grad = (scale * (weighted - query_vec.astype(jnp.float32))).astype(jnp.bfloat16)
    query_back = lax.dot_general(
        query_grad, query_tower, (((1,), (1,)), ((), ())), preferred_element_type=jnp.float32
    )
    item_back = lax.dot_general(
        item_grad, item_tower, (((1,), (1,)), ((), ())), preferred_element_type=jnp.float32
    )
    norm_sq = (
        squares(query_in) * squares(query_grad)
        + squares(item_in) * squares(item_grad)
        + squares(query_back)
        + squares(item_back)
    )
    factor = jnp.minimum(1.0, clip_norm / jnp.sqrt(norm_sq + 1e-06))
    clipped_query = (factor[:, None] * query_grad.astype(jnp.float32)).astype(jnp.bfloat16)
    clipped_item = (factor[:, None] * item_grad.astype(jnp.float32)).astype(jnp.bfloat16)
    tower_part = jnp.stack(
        [
            lax.dot_general(
                query_in,
                clipped_query,
                (((0,), (0,)), ((), ())),
                preferred_element_type=jnp.float32,
            ),
            lax.dot_general(
                item_in, clipped_item, (((0,), (0,)), ((), ())), preferred_element_type=jnp.float32
            ),
        ]
    )
    back_all = jnp.concatenate(
        [query_back.reshape(batch, feats, emb_width), item_back.reshape(batch, feats, emb_width)],
        axis=1,
    )
    lookup_grad = (factor[:, None, None] * back_all).astype(jnp.bfloat16)
    grad_out = lax.dot_general(
        pool_match,
        lookup_grad.reshape(batch * slots, emb_width),
        (((0,), (0,)), ((), ())),
        preferred_element_type=jnp.float32,
    ).astype(jnp.bfloat16)
    grad_in = lax.all_to_all(
        grad_out.reshape(shards, capacity, emb_width),
        "table",
        split_axis=0,
        concat_axis=0,
        tiled=True,
    )
    row_sum = lax.dot_general(
        row_match,
        grad_in.reshape(shards * capacity, emb_width),
        (((0,), (0,)), ((), ())),
        preferred_element_type=jnp.float32,
    )
    row_count = jnp.sum(row_match.astype(jnp.float32), axis=0)
    shard_rows = rows_dev // n_dp
    tower_rows = 2 * hidden_width
    dp_rows = tower_rows // n_dp
    own_rows = dp_rows // shards
    count_lanes = emb_width // shard_rows
    packed = jnp.concatenate(
        [
            tower_part.reshape(n_dp, dp_rows, out_width),
            row_sum.reshape(n_dp, shard_rows, emb_width),
            jnp.broadcast_to(
                row_count.reshape(n_dp, 1, shard_rows, 1), (n_dp, 1, shard_rows, count_lanes)
            ).reshape(n_dp, 1, emb_width),
        ],
        axis=1,
    )
    packed = jnp.sum(lax.all_to_all(packed, "dp", 0, 0, tiled=True), axis=0)
    own_sum = packed[dp_rows : dp_rows + shard_rows]
    own_count = packed[dp_rows + shard_rows].reshape(shard_rows, count_lanes)[:, 0]
    own_seeds = lax.dynamic_slice_in_dim(row_seeds, dp_index * shard_rows, shard_rows)
    own_update = own_sum / clip_norm + NOISE_MULT * jnp.where(
        own_count[:, None] > 0.0, hashed_noise(own_seeds, emb_width), 0.0
    )
    part = packed[:dp_rows].reshape(shards, own_rows, out_width)
    part = jnp.sum(lax.all_to_all(part, "table", 0, 0, tiled=True), axis=0)
    first_row = dp_index * dp_rows + table_index * own_rows
    tower_seed_rows = lax.dynamic_slice_in_dim(tower_seeds.reshape(tower_rows), first_row, own_rows)
    part = part / clip_norm + NOISE_MULT * hashed_noise(tower_seed_rows, out_width)
    part = lax.all_to_all(
        jnp.broadcast_to(part[None], (shards,) + part.shape), "table", 0, 0, tiled=True
    ).reshape(dp_rows, out_width)
    finished = jnp.concatenate([part, own_update], axis=0)
    finished = lax.all_to_all(
        jnp.broadcast_to(finished[None], (n_dp,) + finished.shape), "dp", 0, 0, tiled=True
    )
    tower_update = finished[:, :dp_rows].reshape(2, hidden_width, out_width)
    table_update = finished[:, dp_rows:].reshape(rows_dev, emb_width)
    return (table_update, tower_update)


def solution(mesh):
    in_specs = (P("table", None), P(("dp", "table"), None, None), P(), P(), P(), P("table"), P())
    out_specs = (P("table", None), P())
    return jax.shard_map(body, mesh=mesh, in_specs=in_specs, out_specs=out_specs, check_vma=False)
```

```python
import math

import jax
import jax.numpy as jnp
from jax import lax
from jax.sharding import PartitionSpec as P

NOISE_MULT = 0.1


def hashed_noise(seed_rows, width):
    columns = jnp.arange(width, dtype=jnp.int32)
    summed = jnp.zeros(seed_rows.shape + (width,), jnp.float32)
    for section in range(2):
        mixed = seed_rows[..., None] + (columns * 2 + section) * 1013904223
        mixed = mixed ^ mixed >> 15 & 131071
        mixed = mixed * 73244475
        mixed = mixed ^ mixed >> 13 & 524287
        mixed = mixed * 1597334677
        mixed = mixed ^ mixed >> 16 & 65535
        lower = (mixed & 65535).astype(jnp.float32) / 65536.0 - 0.5
        upper = (mixed >> 16 & 65535).astype(jnp.float32) / 65536.0 - 0.5
        summed = summed + lower + upper
    return summed * math.sqrt(3.0)


def squares(values):
    return jnp.sum(jnp.square(values.astype(jnp.float32)), axis=1)


def body(id_table, lookup_ids, row_owner, query_tower, item_tower, row_seeds, tower_seeds):
    shards = lax.axis_size("table")
    rows_dev, emb_width = id_table.shape
    batch, slots, bags = lookup_ids.shape
    feats = slots // 2
    hidden_width, out_width = query_tower.shape
    scale = 200.0 / math.sqrt(out_width)
    clip_norm = 0.9 * math.sqrt(2.0 * hidden_width + 400.0)
    requests = batch * slots * bags
    capacity = 3 * requests // (2 * shards)
    positions = row_owner[lookup_ids.reshape(-1)]
    owners = positions // rows_dev
    local_rows = positions - owners * rows_dev
    one_hot = owners[:, None] == jnp.arange(shards, dtype=jnp.int32)[None, :]
    order = jnp.arange(requests, dtype=jnp.int32)
    earlier = (order[None, :] < order[:, None]).astype(jnp.bfloat16)
    before = jnp.dot(earlier, one_hot.astype(jnp.bfloat16), preferred_element_type=jnp.float32)
    ranks = jnp.sum(jnp.where(one_hot, before, 0.0), axis=1).astype(jnp.int32)
    targets = owners * capacity + ranks
    slots_all = jnp.arange(shards * capacity, dtype=jnp.int32)
    slot_match = targets[:, None] == slots_all[None, :]
    outgoing = jnp.max(jnp.where(slot_match, local_rows[:, None], -1), axis=0)
    outgoing = outgoing.reshape(shards, capacity)
    incoming = lax.all_to_all(outgoing, "table", split_axis=0, concat_axis=0, tiled=True)
    flat_in = incoming.reshape(-1)
    row_match = (flat_in[:, None] == jnp.arange(rows_dev, dtype=jnp.int32)[None, :]).astype(
        jnp.bfloat16
    )
    fetched = jnp.dot(row_match, id_table, preferred_element_type=jnp.float32).astype(jnp.bfloat16)
    returned = lax.all_to_all(
        fetched.reshape(shards, capacity, emb_width), "table", split_axis=0, concat_axis=0, tiled=True
    )
    pair_targets = targets.reshape(batch * slots, bags)
    pool_match = pair_targets[:, 0:1] == slots_all[None, :]
    for bag in range(1, bags):
        pool_match = pool_match | (pair_targets[:, bag : bag + 1] == slots_all[None, :])
    pool_match = pool_match.astype(jnp.bfloat16)
    pooled = jnp.dot(
        pool_match,
        returned.reshape(shards * capacity, emb_width),
        preferred_element_type=jnp.float32,
    )
    pooled = pooled.astype(jnp.bfloat16).reshape(batch, slots, emb_width)
    query_in = pooled[:, :feats].reshape(batch, hidden_width)
    item_in = pooled[:, feats:].reshape(batch, hidden_width)
    query_vec = jnp.dot(query_in, query_tower, preferred_element_type=jnp.float32).astype(
        jnp.bfloat16
    )
    item_vec = jnp.dot(item_in, item_tower, preferred_element_type=jnp.float32).astype(jnp.bfloat16)
    n_dp = lax.axis_size("dp")
    dp_index = lax.axis_index("dp")
    table_index = lax.axis_index("table")
    both = jnp.concatenate([query_vec, item_vec], axis=1)
    both = lax.all_to_all(
        jnp.broadcast_to(both[None], (n_dp,) + both.shape), "dp", 0, 0, tiled=True
    )
    all_queries = both[:, :, :out_width].reshape(n_dp * batch, out_width)
    all_items = both[:, :, out_width:].reshape(n_dp * batch, out_width)
    scores = scale * lax.dot_general(
        all_queries, all_items, (((1,), (1,)), ((), ())), preferred_element_type=jnp.float32
    )
    peak = jnp.max(scores, axis=1, keepdims=True)
    log_total = peak + jnp.log(jnp.sum(jnp.exp(scores - peak), axis=1, keepdims=True))
    own = dp_index * batch
    row_scores = lax.dynamic_slice_in_dim(scores, own, batch, axis=0)
    row_total = lax.dynamic_slice_in_dim(log_total, own, batch, axis=0)
    col_scores = lax.dynamic_slice_in_dim(scores, own, batch, axis=1)
    row_probs = jnp.exp(row_scores - row_total).astype(jnp.bfloat16)
    col_probs = jnp.exp(col_scores - log_total).astype(jnp.bfloat16)
    query_grad = (
        scale
        * (
            jnp.dot(row_probs, all_items, preferred_element_type=jnp.float32)
            - item_vec.astype(jnp.float32)
        )
    ).astype(jnp.bfloat16)
    weighted = lax.dot_general(
        col_probs, all_queries, (((0,), (0,)), ((), ())), preferred_element_type=jnp.float32
    )
    item_grad = (scale * (weighted - query_vec.astype(jnp.float32))).astype(jnp.bfloat16)
    query_back = lax.dot_general(
        query_grad, query_tower, (((1,), (1,)), ((), ())), preferred_element_type=jnp.float32
    )
    item_back = lax.dot_general(
        item_grad, item_tower, (((1,), (1,)), ((), ())), preferred_element_type=jnp.float32
    )
    norm_sq = (
        squares(query_in) * squares(query_grad)
        + squares(item_in) * squares(item_grad)
        + squares(query_back)
        + squares(item_back)
    )
    factor = jnp.minimum(1.0, clip_norm / jnp.sqrt(norm_sq + 1e-06))
    clipped_query = (factor[:, None] * query_grad.astype(jnp.float32)).astype(jnp.bfloat16)
    clipped_item = (factor[:, None] * item_grad.astype(jnp.float32)).astype(jnp.bfloat16)
    tower_part = jnp.stack(
        [
            lax.dot_general(
                query_in,
                clipped_query,
                (((0,), (0,)), ((), ())),
                preferred_element_type=jnp.float32,
            ),
            lax.dot_general(
                item_in, clipped_item, (((0,), (0,)), ((), ())), preferred_element_type=jnp.float32
            ),
        ]
    )
    back_all = jnp.concatenate(
        [query_back.reshape(batch, feats, emb_width), item_back.reshape(batch, feats, emb_width)],
        axis=1,
    )
    lookup_grad = (factor[:, None, None] * back_all).astype(jnp.bfloat16)
    grad_out = lax.dot_general(
        pool_match,
        lookup_grad.reshape(batch * slots, emb_width),
        (((0,), (0,)), ((), ())),
        preferred_element_type=jnp.float32,
    ).astype(jnp.bfloat16)
    grad_in = lax.all_to_all(
        grad_out.reshape(shards, capacity, emb_width),
        "table",
        split_axis=0,
        concat_axis=0,
        tiled=True,
    )
    row_sum = lax.dot_general(
        row_match,
        grad_in.reshape(shards * capacity, emb_width),
        (((0,), (0,)), ((), ())),
        preferred_element_type=jnp.float32,
    )
    row_count = jnp.sum(row_match.astype(jnp.float32), axis=0)
    shard_rows = rows_dev // n_dp
    tower_rows = 2 * hidden_width
    dp_rows = tower_rows // n_dp
    own_rows = dp_rows // shards
    count_lanes = emb_width // shard_rows
    packed = jnp.concatenate(
        [
            tower_part.reshape(n_dp, dp_rows, out_width),
            row_sum.reshape(n_dp, shard_rows, emb_width),
            jnp.broadcast_to(
                row_count.reshape(n_dp, 1, shard_rows, 1), (n_dp, 1, shard_rows, count_lanes)
            ).reshape(n_dp, 1, emb_width),
        ],
        axis=1,
    )
    packed = jnp.sum(lax.all_to_all(packed, "dp", 0, 0, tiled=True), axis=0)
    own_sum = packed[dp_rows : dp_rows + shard_rows]
    own_count = packed[dp_rows + shard_rows].reshape(shard_rows, count_lanes)[:, 0]
    own_seeds = lax.dynamic_slice_in_dim(row_seeds, dp_index * shard_rows, shard_rows)
    own_update = own_sum / clip_norm + NOISE_MULT * jnp.where(
        own_count[:, None] > 0.0, hashed_noise(own_seeds, emb_width), 0.0
    )
    part = packed[:dp_rows].reshape(shards, own_rows, out_width)
    part = jnp.sum(lax.all_to_all(part, "table", 0, 0, tiled=True), axis=0)
    first_row = dp_index * dp_rows + table_index * own_rows
    tower_seed_rows = lax.dynamic_slice_in_dim(tower_seeds.reshape(tower_rows), first_row, own_rows)
    part = part / clip_norm + NOISE_MULT * hashed_noise(tower_seed_rows, out_width)
    part = lax.all_to_all(
        jnp.broadcast_to(part[None], (shards,) + part.shape), "table", 0, 0, tiled=True
    ).reshape(dp_rows, out_width)
    finished = jnp.concatenate([part, own_update], axis=0).astype(jnp.bfloat16)
    finished = lax.all_to_all(
        jnp.broadcast_to(finished[None], (n_dp,) + finished.shape), "dp", 0, 0, tiled=True
    ).astype(jnp.float32)
    tower_update = finished[:, :dp_rows].reshape(2, hidden_width, out_width)
    table_update = finished[:, dp_rows:].reshape(rows_dev, emb_width)
    return (table_update, tower_update)


def solution(mesh):
    in_specs = (P("table", None), P(("dp", "table"), None, None), P(), P(), P(), P("table"), P())
    out_specs = (P("table", None), P())
    return jax.shard_map(body, mesh=mesh, in_specs=in_specs, out_specs=out_specs, check_vma=False)
```

```python
import math

import jax
import jax.numpy as jnp
from jax import lax
from jax.sharding import PartitionSpec as P

NOISE_MULT = 0.1


def hashed_noise(seed_rows, width):
    columns = jnp.arange(width, dtype=jnp.int32)
    summed = jnp.zeros(seed_rows.shape + (width,), jnp.float32)
    for section in range(2):
        mixed = seed_rows[..., None] + (columns * 2 + section) * 1013904223
        mixed = mixed ^ mixed >> 15 & 131071
        mixed = mixed * 73244475
        mixed = mixed ^ mixed >> 13 & 524287
        mixed = mixed * 1597334677
        mixed = mixed ^ mixed >> 16 & 65535
        lower = (mixed & 65535).astype(jnp.float32) / 65536.0 - 0.5
        upper = (mixed >> 16 & 65535).astype(jnp.float32) / 65536.0 - 0.5
        summed = summed + lower + upper
    return summed * math.sqrt(3.0)


def squares(values):
    return jnp.sum(jnp.square(values.astype(jnp.float32)), axis=1)


def body(id_table, lookup_ids, row_owner, query_tower, item_tower, row_seeds, tower_seeds):
    shards = lax.axis_size("table")
    rows_dev, emb_width = id_table.shape
    batch, slots, bags = lookup_ids.shape
    feats = slots // 2
    hidden_width, out_width = query_tower.shape
    scale = 200.0 / math.sqrt(out_width)
    clip_norm = 0.9 * math.sqrt(2.0 * hidden_width + 400.0)
    requests = batch * slots * bags
    capacity = 3 * requests // (2 * shards)
    positions = row_owner[lookup_ids.reshape(-1)]
    owners = positions // rows_dev
    local_rows = positions - owners * rows_dev
    one_hot = owners[:, None] == jnp.arange(shards, dtype=jnp.int32)[None, :]
    order = jnp.arange(requests, dtype=jnp.int32)
    earlier = (order[None, :] < order[:, None]).astype(jnp.bfloat16)
    before = jnp.dot(earlier, one_hot.astype(jnp.bfloat16), preferred_element_type=jnp.float32)
    ranks = jnp.sum(jnp.where(one_hot, before, 0.0), axis=1).astype(jnp.int32)
    targets = owners * capacity + ranks
    slots_all = jnp.arange(shards * capacity, dtype=jnp.int32)
    slot_match = targets[:, None] == slots_all[None, :]
    outgoing = jnp.max(jnp.where(slot_match, local_rows[:, None], -1), axis=0)
    outgoing = outgoing.reshape(shards, capacity)
    incoming = lax.all_to_all(outgoing, "table", split_axis=0, concat_axis=0, tiled=True)
    flat_in = incoming.reshape(-1)
    row_match = (flat_in[:, None] == jnp.arange(rows_dev, dtype=jnp.int32)[None, :]).astype(
        jnp.bfloat16
    )
    fetched = jnp.dot(row_match, id_table, preferred_element_type=jnp.float32).astype(jnp.bfloat16)
    returned = lax.all_to_all(
        fetched.reshape(shards, capacity, emb_width), "table", split_axis=0, concat_axis=0, tiled=True
    )
    pair_targets = targets.reshape(batch * slots, bags)
    pool_match = pair_targets[:, 0:1] == slots_all[None, :]
    for bag in range(1, bags):
        pool_match = pool_match | (pair_targets[:, bag : bag + 1] == slots_all[None, :])
    pool_match = pool_match.astype(jnp.bfloat16)
    pooled = jnp.dot(
        pool_match,
        returned.reshape(shards * capacity, emb_width),
        preferred_element_type=jnp.float32,
    )
    pooled = pooled.astype(jnp.bfloat16).reshape(batch, slots, emb_width)
    query_in = pooled[:, :feats].reshape(batch, hidden_width)
    item_in = pooled[:, feats:].reshape(batch, hidden_width)
    query_vec = jnp.dot(query_in, query_tower, preferred_element_type=jnp.float32).astype(
        jnp.bfloat16
    )
    item_vec = jnp.dot(item_in, item_tower, preferred_element_type=jnp.float32).astype(jnp.bfloat16)
    n_dp = lax.axis_size("dp")
    dp_index = lax.axis_index("dp")
    table_index = lax.axis_index("table")
    both = jnp.concatenate([query_vec, item_vec], axis=1)
    both = lax.all_to_all(
        jnp.broadcast_to(both[None], (n_dp,) + both.shape), "dp", 0, 0, tiled=True
    )
    all_queries = both[:, :, :out_width].reshape(n_dp * batch, out_width)
    all_items = both[:, :, out_width:].reshape(n_dp * batch, out_width)
    scores = scale * lax.dot_general(
        all_queries, all_items, (((1,), (1,)), ((), ())), preferred_element_type=jnp.float32
    )
    peak = jnp.max(scores, axis=1, keepdims=True)
    log_total = peak + jnp.log(jnp.sum(jnp.exp(scores - peak), axis=1, keepdims=True))
    own = dp_index * batch
    row_scores = lax.dynamic_slice_in_dim(scores, own, batch, axis=0)
    row_total = lax.dynamic_slice_in_dim(log_total, own, batch, axis=0)
    col_scores = lax.dynamic_slice_in_dim(scores, own, batch, axis=1)
    row_probs = jnp.exp(row_scores - row_total).astype(jnp.bfloat16)
    col_probs = jnp.exp(col_scores - log_total).astype(jnp.bfloat16)
    query_grad = (
        scale
        * (
            jnp.dot(row_probs, all_items, preferred_element_type=jnp.float32)
            - item_vec.astype(jnp.float32)
        )
    ).astype(jnp.bfloat16)
    weighted = lax.dot_general(
        col_probs, all_queries, (((0,), (0,)), ((), ())), preferred_element_type=jnp.float32
    )
    item_grad = (scale * (weighted - query_vec.astype(jnp.float32))).astype(jnp.bfloat16)
    query_back = lax.dot_general(
        query_grad, query_tower, (((1,), (1,)), ((), ())), preferred_element_type=jnp.float32
    )
    item_back = lax.dot_general(
        item_grad, item_tower, (((1,), (1,)), ((), ())), preferred_element_type=jnp.float32
    )
    norm_sq = (
        squares(query_in) * squares(query_grad)
        + squares(item_in) * squares(item_grad)
        + squares(query_back)
        + squares(item_back)
    )
    factor = jnp.minimum(1.0, clip_norm / jnp.sqrt(norm_sq + 1e-06))
    clipped_query = (factor[:, None] * query_grad.astype(jnp.float32)).astype(jnp.bfloat16)
    clipped_item = (factor[:, None] * item_grad.astype(jnp.float32)).astype(jnp.bfloat16)
    tower_part = jnp.stack(
        [
            lax.dot_general(
                query_in,
                clipped_query,
                (((0,), (0,)), ((), ())),
                preferred_element_type=jnp.float32,
            ),
            lax.dot_general(
                item_in, clipped_item, (((0,), (0,)), ((), ())), preferred_element_type=jnp.float32
            ),
        ]
    )
    back_all = jnp.concatenate(
        [query_back.reshape(batch, feats, emb_width), item_back.reshape(batch, feats, emb_width)],
        axis=1,
    )
    lookup_grad = (factor[:, None, None] * back_all).astype(jnp.bfloat16)
    grad_out = lax.dot_general(
        pool_match,
        lookup_grad.reshape(batch * slots, emb_width),
        (((0,), (0,)), ((), ())),
        preferred_element_type=jnp.float32,
    ).astype(jnp.bfloat16)
    grad_in = lax.all_to_all(
        grad_out.reshape(shards, capacity, emb_width),
        "table",
        split_axis=0,
        concat_axis=0,
        tiled=True,
    )
    row_sum = lax.dot_general(
        row_match,
        grad_in.reshape(shards * capacity, emb_width),
        (((0,), (0,)), ((), ())),
        preferred_element_type=jnp.float32,
    )
    row_count = jnp.sum(row_match.astype(jnp.float32), axis=0)
    shard_rows = rows_dev // n_dp
    tower_rows = 2 * hidden_width
    dp_rows = tower_rows // n_dp
    own_rows = dp_rows // shards
    count_lanes = emb_width // shard_rows
    tower_slice = lax.psum_scatter(
        tower_part.reshape(tower_rows, out_width), "dp", scatter_dimension=0, tiled=True
    )
    packed = jnp.concatenate(
        [
            row_sum.reshape(n_dp, shard_rows, emb_width),
            jnp.broadcast_to(
                row_count.reshape(n_dp, 1, shard_rows, 1), (n_dp, 1, shard_rows, count_lanes)
            ).reshape(n_dp, 1, emb_width),
        ],
        axis=1,
    )
    packed = jnp.sum(lax.all_to_all(packed, "dp", 0, 0, tiled=True), axis=0)
    own_sum = packed[:shard_rows]
    own_count = packed[shard_rows].reshape(shard_rows, count_lanes)[:, 0]
    own_seeds = lax.dynamic_slice_in_dim(row_seeds, dp_index * shard_rows, shard_rows)
    own_update = own_sum / clip_norm + NOISE_MULT * jnp.where(
        own_count[:, None] > 0.0, hashed_noise(own_seeds, emb_width), 0.0
    )
    part = tower_slice.reshape(shards, own_rows, out_width)
    part = jnp.sum(lax.all_to_all(part, "table", 0, 0, tiled=True), axis=0)
    first_row = dp_index * dp_rows + table_index * own_rows
    tower_seed_rows = lax.dynamic_slice_in_dim(tower_seeds.reshape(tower_rows), first_row, own_rows)
    part = part / clip_norm + NOISE_MULT * hashed_noise(tower_seed_rows, out_width)
    part = lax.all_to_all(
        jnp.broadcast_to(part[None], (shards,) + part.shape), "table", 0, 0, tiled=True
    ).reshape(dp_rows, out_width)
    finished = jnp.concatenate([part, own_update], axis=0).astype(jnp.bfloat16)
    finished = lax.all_to_all(
        jnp.broadcast_to(finished[None], (n_dp,) + finished.shape), "dp", 0, 0, tiled=True
    ).astype(jnp.float32)
    tower_update = finished[:, :dp_rows].reshape(2, hidden_width, out_width)
    table_update = finished[:, dp_rows:].reshape(rows_dev, emb_width)
    return (table_update, tower_update)


def solution(mesh):
    in_specs = (P("table", None), P(("dp", "table"), None, None), P(), P(), P(), P("table"), P())
    out_specs = (P("table", None), P())
    return jax.shard_map(body, mesh=mesh, in_specs=in_specs, out_specs=out_specs, check_vma=False)
```

```python
import math

import jax
import jax.numpy as jnp
from jax import lax
from jax.sharding import PartitionSpec as P

NOISE_MULT = 0.1


def hashed_noise(seed_rows, width):
    columns = jnp.arange(width, dtype=jnp.int32)
    summed = jnp.zeros(seed_rows.shape + (width,), jnp.float32)
    for section in range(2):
        mixed = seed_rows[..., None] + (columns * 2 + section) * 1013904223
        mixed = mixed ^ mixed >> 15 & 131071
        mixed = mixed * 73244475
        mixed = mixed ^ mixed >> 13 & 524287
        mixed = mixed * 1597334677
        mixed = mixed ^ mixed >> 16 & 65535
        lower = (mixed & 65535).astype(jnp.float32) / 65536.0 - 0.5
        upper = (mixed >> 16 & 65535).astype(jnp.float32) / 65536.0 - 0.5
        summed = summed + lower + upper
    return summed * math.sqrt(3.0)


def squares(values):
    return jnp.sum(jnp.square(values.astype(jnp.float32)), axis=1)


def body(id_table, lookup_ids, row_owner, query_tower, item_tower, row_seeds, tower_seeds):
    shards = lax.axis_size("table")
    rows_dev, emb_width = id_table.shape
    batch, slots, bags = lookup_ids.shape
    feats = slots // 2
    hidden_width, out_width = query_tower.shape
    scale = 200.0 / math.sqrt(out_width)
    clip_norm = 0.9 * math.sqrt(2.0 * hidden_width + 400.0)
    requests = batch * slots * bags
    capacity = 3 * requests // (2 * shards)
    flat_ids = lookup_ids.reshape(-1)
    lane_width = 128
    owner_blocks = row_owner.reshape(-1, lane_width)
    block_match = (
        (flat_ids // lane_width)[:, None]
        == jnp.arange(owner_blocks.shape[0], dtype=jnp.int32)[None, :]
    ).astype(jnp.bfloat16)
    owner_high = jnp.dot(
        block_match, (owner_blocks // 256).astype(jnp.bfloat16), preferred_element_type=jnp.float32
    )
    owner_low = jnp.dot(
        block_match, (owner_blocks % 256).astype(jnp.bfloat16), preferred_element_type=jnp.float32
    )
    lane_match = (flat_ids % lane_width)[:, None] == jnp.arange(lane_width, dtype=jnp.int32)[None, :]
    positions = jnp.sum(
        jnp.where(lane_match, owner_high.astype(jnp.int32) * 256 + owner_low.astype(jnp.int32), 0),
        axis=1,
    )
    owners = positions // rows_dev
    local_rows = positions - owners * rows_dev
    one_hot = owners[:, None] == jnp.arange(shards, dtype=jnp.int32)[None, :]
    order = jnp.arange(requests, dtype=jnp.int32)
    earlier = (order[None, :] < order[:, None]).astype(jnp.bfloat16)
    before = jnp.dot(earlier, one_hot.astype(jnp.bfloat16), preferred_element_type=jnp.float32)
    ranks = jnp.sum(jnp.where(one_hot, before, 0.0), axis=1).astype(jnp.int32)
    targets = owners * capacity + ranks
    slots_all = jnp.arange(shards * capacity, dtype=jnp.int32)
    slot_match = targets[:, None] == slots_all[None, :]
    row_parts = jnp.stack(
        [local_rows // 32, local_rows % 32, jnp.ones_like(local_rows)], axis=1
    ).astype(jnp.bfloat16)
    slot_parts = lax.dot_general(
        slot_match.astype(jnp.bfloat16),
        row_parts,
        (((0,), (0,)), ((), ())),
        preferred_element_type=jnp.float32,
    ).astype(jnp.int32)
    outgoing = jnp.where(
        slot_parts[:, 2] > 0, slot_parts[:, 0] * 32 + slot_parts[:, 1], -1
    )
    outgoing = outgoing.reshape(shards, capacity)
    incoming = lax.all_to_all(outgoing, "table", split_axis=0, concat_axis=0, tiled=True)
    flat_in = incoming.reshape(-1)
    row_match = (flat_in[:, None] == jnp.arange(rows_dev, dtype=jnp.int32)[None, :]).astype(
        jnp.bfloat16
    )
    fetched = jnp.dot(row_match, id_table, preferred_element_type=jnp.float32).astype(jnp.bfloat16)
    returned = lax.all_to_all(
        fetched.reshape(shards, capacity, emb_width), "table", split_axis=0, concat_axis=0, tiled=True
    )
    pair_targets = targets.reshape(batch * slots, bags)
    pool_match = pair_targets[:, 0:1] == slots_all[None, :]
    for bag in range(1, bags):
        pool_match = pool_match | (pair_targets[:, bag : bag + 1] == slots_all[None, :])
    pool_match = pool_match.astype(jnp.bfloat16)
    pooled = jnp.dot(
        pool_match,
        returned.reshape(shards * capacity, emb_width),
        preferred_element_type=jnp.float32,
    )
    pooled = pooled.astype(jnp.bfloat16).reshape(batch, slots, emb_width)
    query_in = pooled[:, :feats].reshape(batch, hidden_width)
    item_in = pooled[:, feats:].reshape(batch, hidden_width)
    query_vec = jnp.dot(query_in, query_tower, preferred_element_type=jnp.float32).astype(
        jnp.bfloat16
    )
    item_vec = jnp.dot(item_in, item_tower, preferred_element_type=jnp.float32).astype(jnp.bfloat16)
    n_dp = lax.axis_size("dp")
    dp_index = lax.axis_index("dp")
    table_index = lax.axis_index("table")
    both = jnp.concatenate([query_vec, item_vec], axis=1)
    both = lax.all_to_all(
        jnp.broadcast_to(both[None], (n_dp,) + both.shape), "dp", 0, 0, tiled=True
    )
    all_queries = both[:, :, :out_width].reshape(n_dp * batch, out_width)
    all_items = both[:, :, out_width:].reshape(n_dp * batch, out_width)
    scores = scale * lax.dot_general(
        all_queries, all_items, (((1,), (1,)), ((), ())), preferred_element_type=jnp.float32
    )
    peak = jnp.max(scores, axis=1, keepdims=True)
    log_total = peak + jnp.log(jnp.sum(jnp.exp(scores - peak), axis=1, keepdims=True))
    own = dp_index * batch
    row_scores = lax.dynamic_slice_in_dim(scores, own, batch, axis=0)
    row_total = lax.dynamic_slice_in_dim(log_total, own, batch, axis=0)
    col_scores = lax.dynamic_slice_in_dim(scores, own, batch, axis=1)
    row_probs = jnp.exp(row_scores - row_total).astype(jnp.bfloat16)
    col_probs = jnp.exp(col_scores - log_total).astype(jnp.bfloat16)
    query_grad = (
        scale
        * (
            jnp.dot(row_probs, all_items, preferred_element_type=jnp.float32)
            - item_vec.astype(jnp.float32)
        )
    ).astype(jnp.bfloat16)
    weighted = lax.dot_general(
        col_probs, all_queries, (((0,), (0,)), ((), ())), preferred_element_type=jnp.float32
    )
    item_grad = (scale * (weighted - query_vec.astype(jnp.float32))).astype(jnp.bfloat16)
    query_back = lax.dot_general(
        query_grad, query_tower, (((1,), (1,)), ((), ())), preferred_element_type=jnp.float32
    )
    item_back = lax.dot_general(
        item_grad, item_tower, (((1,), (1,)), ((), ())), preferred_element_type=jnp.float32
    )
    norm_sq = (
        squares(query_in) * squares(query_grad)
        + squares(item_in) * squares(item_grad)
        + squares(query_back)
        + squares(item_back)
    )
    factor = jnp.minimum(1.0, clip_norm / jnp.sqrt(norm_sq + 1e-06))
    clipped_query = (factor[:, None] * query_grad.astype(jnp.float32)).astype(jnp.bfloat16)
    clipped_item = (factor[:, None] * item_grad.astype(jnp.float32)).astype(jnp.bfloat16)
    tower_part = jnp.stack(
        [
            lax.dot_general(
                query_in,
                clipped_query,
                (((0,), (0,)), ((), ())),
                preferred_element_type=jnp.float32,
            ),
            lax.dot_general(
                item_in, clipped_item, (((0,), (0,)), ((), ())), preferred_element_type=jnp.float32
            ),
        ]
    )
    back_all = jnp.concatenate(
        [query_back.reshape(batch, feats, emb_width), item_back.reshape(batch, feats, emb_width)],
        axis=1,
    )
    lookup_grad = (factor[:, None, None] * back_all).astype(jnp.bfloat16)
    grad_out = lax.dot_general(
        pool_match,
        lookup_grad.reshape(batch * slots, emb_width),
        (((0,), (0,)), ((), ())),
        preferred_element_type=jnp.float32,
    ).astype(jnp.bfloat16)
    grad_in = lax.all_to_all(
        grad_out.reshape(shards, capacity, emb_width),
        "table",
        split_axis=0,
        concat_axis=0,
        tiled=True,
    )
    row_sum = lax.dot_general(
        row_match,
        grad_in.reshape(shards * capacity, emb_width),
        (((0,), (0,)), ((), ())),
        preferred_element_type=jnp.float32,
    )
    row_count = jnp.sum(row_match.astype(jnp.float32), axis=0)
    shard_rows = rows_dev // n_dp
    tower_rows = 2 * hidden_width
    dp_rows = tower_rows // n_dp
    own_rows = dp_rows // shards
    count_lanes = emb_width // shard_rows
    packed = jnp.concatenate(
        [
            tower_part.reshape(n_dp, dp_rows, out_width),
            row_sum.reshape(n_dp, shard_rows, emb_width),
            jnp.broadcast_to(
                row_count.reshape(n_dp, 1, shard_rows, 1), (n_dp, 1, shard_rows, count_lanes)
            ).reshape(n_dp, 1, emb_width),
        ],
        axis=1,
    )
    packed = jnp.sum(lax.all_to_all(packed, "dp", 0, 0, tiled=True), axis=0)
    own_sum = packed[dp_rows : dp_rows + shard_rows]
    own_count = packed[dp_rows + shard_rows].reshape(shard_rows, count_lanes)[:, 0]
    own_seeds = lax.dynamic_slice_in_dim(row_seeds, dp_index * shard_rows, shard_rows)
    own_update = own_sum / clip_norm + NOISE_MULT * jnp.where(
        own_count[:, None] > 0.0, hashed_noise(own_seeds, emb_width), 0.0
    )
    part = packed[:dp_rows].reshape(shards, own_rows, out_width)
    part = jnp.sum(lax.all_to_all(part, "table", 0, 0, tiled=True), axis=0)
    first_row = dp_index * dp_rows + table_index * own_rows
    tower_seed_rows = lax.dynamic_slice_in_dim(tower_seeds.reshape(tower_rows), first_row, own_rows)
    part = part / clip_norm + NOISE_MULT * hashed_noise(tower_seed_rows, out_width)
    part = lax.all_to_all(
        jnp.broadcast_to(part[None], (shards,) + part.shape), "table", 0, 0, tiled=True
    ).reshape(dp_rows, out_width)
    finished = jnp.concatenate([part, own_update], axis=0).astype(jnp.bfloat16)
    finished = lax.all_to_all(
        jnp.broadcast_to(finished[None], (n_dp,) + finished.shape), "dp", 0, 0, tiled=True
    ).astype(jnp.float32)
    tower_update = finished[:, :dp_rows].reshape(2, hidden_width, out_width)
    table_update = finished[:, dp_rows:].reshape(rows_dev, emb_width)
    return (table_update, tower_update)


def solution(mesh):
    in_specs = (P("table", None), P(("dp", "table"), None, None), P(), P(), P(), P("table"), P())
    out_specs = (P("table", None), P())
    return jax.shard_map(body, mesh=mesh, in_specs=in_specs, out_specs=out_specs, check_vma=False)
```

```python
import math

import jax
import jax.numpy as jnp
from jax import lax
from jax.sharding import PartitionSpec as P

NOISE_MULT = 0.1


def hashed_noise(seed_rows, width):
    columns = jnp.arange(width, dtype=jnp.int32)
    summed = jnp.zeros(seed_rows.shape + (width,), jnp.float32)
    for section in range(2):
        mixed = seed_rows[..., None] + (columns * 2 + section) * 1013904223
        mixed = mixed ^ mixed >> 15 & 131071
        mixed = mixed * 73244475
        mixed = mixed ^ mixed >> 13 & 524287
        mixed = mixed * 1597334677
        mixed = mixed ^ mixed >> 16 & 65535
        lower = (mixed & 65535).astype(jnp.float32) / 65536.0 - 0.5
        upper = (mixed >> 16 & 65535).astype(jnp.float32) / 65536.0 - 0.5
        summed = summed + lower + upper
    return summed * math.sqrt(3.0)


def squares(values):
    return jnp.sum(jnp.square(values.astype(jnp.float32)), axis=1)


def body(id_table, lookup_ids, row_owner, query_tower, item_tower, row_seeds, tower_seeds):
    shards = lax.axis_size("table")
    rows_dev, emb_width = id_table.shape
    batch, slots, bags = lookup_ids.shape
    feats = slots // 2
    hidden_width, out_width = query_tower.shape
    scale = 200.0 / math.sqrt(out_width)
    clip_norm = 0.9 * math.sqrt(2.0 * hidden_width + 400.0)
    requests = batch * slots * bags
    capacity = 3 * requests // (2 * shards)
    flat_ids = lookup_ids.reshape(-1)
    lane_width = 128
    owner_blocks = row_owner.reshape(-1, lane_width)
    block_match = (
        (flat_ids // lane_width)[:, None]
        == jnp.arange(owner_blocks.shape[0], dtype=jnp.int32)[None, :]
    ).astype(jnp.bfloat16)
    owner_high = jnp.dot(
        block_match, (owner_blocks // 256).astype(jnp.bfloat16), preferred_element_type=jnp.float32
    )
    owner_low = jnp.dot(
        block_match, (owner_blocks % 256).astype(jnp.bfloat16), preferred_element_type=jnp.float32
    )
    lane_match = (flat_ids % lane_width)[:, None] == jnp.arange(lane_width, dtype=jnp.int32)[None, :]
    positions = jnp.sum(
        jnp.where(lane_match, owner_high.astype(jnp.int32) * 256 + owner_low.astype(jnp.int32), 0),
        axis=1,
    )
    owners = positions // rows_dev
    local_rows = positions - owners * rows_dev
    one_hot = owners[:, None] == jnp.arange(shards, dtype=jnp.int32)[None, :]
    order = jnp.arange(requests, dtype=jnp.int32)
    earlier = (order[None, :] < order[:, None]).astype(jnp.bfloat16)
    before = jnp.dot(earlier, one_hot.astype(jnp.bfloat16), preferred_element_type=jnp.float32)
    ranks = jnp.sum(jnp.where(one_hot, before, 0.0), axis=1).astype(jnp.int32)
    targets = owners * capacity + ranks
    slots_all = jnp.arange(shards * capacity, dtype=jnp.int32)
    slot_match = targets[:, None] == slots_all[None, :]
    row_parts = jnp.stack(
        [local_rows // 32, local_rows % 32, jnp.ones_like(local_rows)], axis=1
    ).astype(jnp.bfloat16)
    slot_parts = lax.dot_general(
        slot_match.astype(jnp.bfloat16),
        row_parts,
        (((0,), (0,)), ((), ())),
        preferred_element_type=jnp.float32,
    ).astype(jnp.int32)
    outgoing = jnp.where(
        slot_parts[:, 2] > 0, slot_parts[:, 0] * 32 + slot_parts[:, 1], -1
    )
    outgoing = outgoing.reshape(shards, capacity)
    incoming = lax.all_to_all(outgoing, "table", split_axis=0, concat_axis=0, tiled=True)
    flat_in = incoming.reshape(-1)
    row_match = (flat_in[:, None] == jnp.arange(rows_dev, dtype=jnp.int32)[None, :]).astype(
        jnp.bfloat16
    )
    fetched = jnp.dot(row_match, id_table, preferred_element_type=jnp.float32).astype(jnp.bfloat16)
    returned = lax.all_to_all(
        fetched.reshape(shards, capacity, emb_width), "table", split_axis=0, concat_axis=0, tiled=True
    )
    pair_targets = targets.reshape(batch * slots, bags)
    pool_match = pair_targets[:, 0:1] == slots_all[None, :]
    for bag in range(1, bags):
        pool_match = pool_match | (pair_targets[:, bag : bag + 1] == slots_all[None, :])
    pool_match = pool_match.astype(jnp.bfloat16)
    pooled = jnp.dot(
        pool_match,
        returned.reshape(shards * capacity, emb_width),
        preferred_element_type=jnp.float32,
    )
    pooled = pooled.astype(jnp.bfloat16).reshape(batch, slots, emb_width)
    query_in = pooled[:, :feats].reshape(batch, hidden_width)
    item_in = pooled[:, feats:].reshape(batch, hidden_width)
    query_vec = jnp.dot(query_in, query_tower, preferred_element_type=jnp.float32).astype(
        jnp.bfloat16
    )
    item_vec = jnp.dot(item_in, item_tower, preferred_element_type=jnp.float32).astype(jnp.bfloat16)
    n_dp = lax.axis_size("dp")
    dp_index = lax.axis_index("dp")
    table_index = lax.axis_index("table")
    both = jnp.concatenate([query_vec, item_vec], axis=1)
    both = lax.all_to_all(
        jnp.broadcast_to(both[None], (n_dp,) + both.shape), "dp", 0, 0, tiled=True
    )
    all_queries = both[:, :, :out_width].reshape(n_dp * batch, out_width)
    all_items = both[:, :, out_width:].reshape(n_dp * batch, out_width)
    scores = scale * lax.dot_general(
        all_queries, all_items, (((1,), (1,)), ((), ())), preferred_element_type=jnp.float32
    )
    peak = jnp.max(scores, axis=1, keepdims=True)
    log_total = peak + jnp.log(jnp.sum(jnp.exp(scores - peak), axis=1, keepdims=True))
    own = dp_index * batch
    row_scores = lax.dynamic_slice_in_dim(scores, own, batch, axis=0)
    row_total = lax.dynamic_slice_in_dim(log_total, own, batch, axis=0)
    col_scores = lax.dynamic_slice_in_dim(scores, own, batch, axis=1)
    row_probs = jnp.exp(row_scores - row_total).astype(jnp.bfloat16)
    col_probs = jnp.exp(col_scores - log_total).astype(jnp.bfloat16)
    query_grad = (
        scale
        * (
            jnp.dot(row_probs, all_items, preferred_element_type=jnp.float32)
            - item_vec.astype(jnp.float32)
        )
    ).astype(jnp.bfloat16)
    weighted = lax.dot_general(
        col_probs, all_queries, (((0,), (0,)), ((), ())), preferred_element_type=jnp.float32
    )
    item_grad = (scale * (weighted - query_vec.astype(jnp.float32))).astype(jnp.bfloat16)
    query_back = lax.dot_general(
        query_grad, query_tower, (((1,), (1,)), ((), ())), preferred_element_type=jnp.float32
    )
    item_back = lax.dot_general(
        item_grad, item_tower, (((1,), (1,)), ((), ())), preferred_element_type=jnp.float32
    )
    norm_sq = (
        squares(query_in) * squares(query_grad)
        + squares(item_in) * squares(item_grad)
        + squares(query_back)
        + squares(item_back)
    )
    factor = jnp.minimum(1.0, clip_norm / jnp.sqrt(norm_sq + 1e-06))
    clipped_query = (factor[:, None] * query_grad.astype(jnp.float32)).astype(jnp.bfloat16)
    clipped_item = (factor[:, None] * item_grad.astype(jnp.float32)).astype(jnp.bfloat16)
    tower_part = jnp.stack(
        [
            lax.dot_general(
                query_in,
                clipped_query,
                (((0,), (0,)), ((), ())),
                preferred_element_type=jnp.float32,
            ),
            lax.dot_general(
                item_in, clipped_item, (((0,), (0,)), ((), ())), preferred_element_type=jnp.float32
            ),
        ]
    )
    back_all = jnp.concatenate(
        [query_back.reshape(batch, feats, emb_width), item_back.reshape(batch, feats, emb_width)],
        axis=1,
    )
    lookup_grad = (factor[:, None, None] * back_all).astype(jnp.bfloat16)
    grad_out = lax.dot_general(
        pool_match,
        lookup_grad.reshape(batch * slots, emb_width),
        (((0,), (0,)), ((), ())),
        preferred_element_type=jnp.float32,
    ).astype(jnp.bfloat16)
    grad_in = lax.all_to_all(
        grad_out.reshape(shards, capacity, emb_width),
        "table",
        split_axis=0,
        concat_axis=0,
        tiled=True,
    )
    row_sum = lax.dot_general(
        row_match,
        grad_in.reshape(shards * capacity, emb_width),
        (((0,), (0,)), ((), ())),
        preferred_element_type=jnp.float32,
    )
    row_count = jnp.sum(row_match.astype(jnp.float32), axis=0)
    shard_rows = rows_dev // n_dp
    count_lanes = emb_width // shard_rows
    core = table_index % 2
    partner = [(i, i ^ 1) for i in range(shards)]
    kept = jnp.where(core == 0, tower_part[0], tower_part[1])
    sent = jnp.where(core == 0, tower_part[1], tower_part[0])
    chip_sum = kept + lax.ppermute(sent, "table", partner)
    dp_rows = hidden_width // n_dp
    chips = shards // 2
    own_rows = dp_rows // chips
    packed = jnp.concatenate(
        [
            chip_sum.reshape(n_dp, dp_rows, out_width),
            row_sum.reshape(n_dp, shard_rows, emb_width),
            jnp.broadcast_to(
                row_count.reshape(n_dp, 1, shard_rows, 1), (n_dp, 1, shard_rows, count_lanes)
            ).reshape(n_dp, 1, emb_width),
        ],
        axis=1,
    )
    packed = jnp.sum(lax.all_to_all(packed, "dp", 0, 0, tiled=True), axis=0)
    own_sum = packed[dp_rows : dp_rows + shard_rows]
    own_count = packed[dp_rows + shard_rows].reshape(shard_rows, count_lanes)[:, 0]
    own_seeds = lax.dynamic_slice_in_dim(row_seeds, dp_index * shard_rows, shard_rows)
    own_update = own_sum / clip_norm + NOISE_MULT * jnp.where(
        own_count[:, None] > 0.0, hashed_noise(own_seeds, emb_width), 0.0
    )
    chunks = packed[:dp_rows].reshape(chips, 1, own_rows, out_width)
    same_core = jnp.arange(2, dtype=jnp.int32)[None, :, None, None] == core
    part = jnp.where(same_core, chunks, 0.0).reshape(shards, own_rows, out_width)
    part = jnp.sum(lax.all_to_all(part, "table", 0, 0, tiled=True), axis=0)
    first_row = core * hidden_width + dp_index * dp_rows + (table_index // 2) * own_rows
    tower_seed_rows = lax.dynamic_slice_in_dim(
        tower_seeds.reshape(2 * hidden_width), first_row, own_rows
    )
    part = part / clip_norm + NOISE_MULT * hashed_noise(tower_seed_rows, out_width)
    part = lax.all_to_all(
        jnp.broadcast_to(part[None], (shards,) + part.shape), "table", 0, 0, tiled=True
    )
    part = part.reshape(chips, 2, own_rows, out_width).transpose(1, 0, 2, 3)
    part = part.reshape(2 * dp_rows, out_width)
    finished = jnp.concatenate([part, own_update], axis=0).astype(jnp.bfloat16)
    finished = lax.all_to_all(
        jnp.broadcast_to(finished[None], (n_dp,) + finished.shape), "dp", 0, 0, tiled=True
    ).astype(jnp.float32)
    tower_update = finished[:, : 2 * dp_rows].reshape(n_dp, 2, dp_rows, out_width)
    tower_update = tower_update.transpose(1, 0, 2, 3).reshape(2, hidden_width, out_width)
    table_update = finished[:, 2 * dp_rows :].reshape(rows_dev, emb_width)
    return (table_update, tower_update)


def solution(mesh):
    in_specs = (P("table", None), P(("dp", "table"), None, None), P(), P(), P(), P("table"), P())
    out_specs = (P("table", None), P())
    return jax.shard_map(body, mesh=mesh, in_specs=in_specs, out_specs=out_specs, check_vma=False)
```

```python
import math

import jax
import jax.numpy as jnp
from jax import lax
from jax.sharding import PartitionSpec as P

NOISE_MULT = 0.1


def hashed_noise(seed_rows, width):
    columns = jnp.arange(width, dtype=jnp.int32)
    summed = jnp.zeros(seed_rows.shape + (width,), jnp.float32)
    for section in range(2):
        mixed = seed_rows[..., None] + (columns * 2 + section) * 1013904223
        mixed = mixed ^ mixed >> 15 & 131071
        mixed = mixed * 73244475
        mixed = mixed ^ mixed >> 13 & 524287
        mixed = mixed * 1597334677
        mixed = mixed ^ mixed >> 16 & 65535
        lower = (mixed & 65535).astype(jnp.float32) / 65536.0 - 0.5
        upper = (mixed >> 16 & 65535).astype(jnp.float32) / 65536.0 - 0.5
        summed = summed + lower + upper
    return summed * math.sqrt(3.0)


def squares(values):
    return jnp.sum(jnp.square(values.astype(jnp.float32)), axis=1)


def body(id_table, lookup_ids, row_owner, query_tower, item_tower, row_seeds, tower_seeds):
    shards = lax.axis_size("table")
    rows_dev, emb_width = id_table.shape
    batch, slots, bags = lookup_ids.shape
    feats = slots // 2
    hidden_width, out_width = query_tower.shape
    scale = 200.0 / math.sqrt(out_width)
    clip_norm = 0.9 * math.sqrt(2.0 * hidden_width + 400.0)
    requests = batch * slots * bags
    capacity = 3 * requests // (2 * shards)
    flat_ids = lookup_ids.reshape(-1)
    lane_width = 128
    owner_blocks = row_owner.reshape(-1, lane_width)
    block_match = (
        (flat_ids // lane_width)[:, None]
        == jnp.arange(owner_blocks.shape[0], dtype=jnp.int32)[None, :]
    ).astype(jnp.bfloat16)
    owner_high = jnp.dot(
        block_match, (owner_blocks // 256).astype(jnp.bfloat16), preferred_element_type=jnp.float32
    )
    owner_low = jnp.dot(
        block_match, (owner_blocks % 256).astype(jnp.bfloat16), preferred_element_type=jnp.float32
    )
    lane_match = (flat_ids % lane_width)[:, None] == jnp.arange(lane_width, dtype=jnp.int32)[None, :]
    positions = jnp.sum(
        jnp.where(lane_match, owner_high.astype(jnp.int32) * 256 + owner_low.astype(jnp.int32), 0),
        axis=1,
    )
    owners = positions // rows_dev
    local_rows = positions - owners * rows_dev
    one_hot = owners[:, None] == jnp.arange(shards, dtype=jnp.int32)[None, :]
    order = jnp.arange(requests, dtype=jnp.int32)
    earlier = (order[None, :] < order[:, None]).astype(jnp.bfloat16)
    before = jnp.dot(earlier, one_hot.astype(jnp.bfloat16), preferred_element_type=jnp.float32)
    ranks = jnp.sum(jnp.where(one_hot, before, 0.0), axis=1).astype(jnp.int32)
    targets = owners * capacity + ranks
    slots_all = jnp.arange(shards * capacity, dtype=jnp.int32)
    slot_match = targets[:, None] == slots_all[None, :]
    row_parts = jnp.stack(
        [local_rows // 32, local_rows % 32, jnp.ones_like(local_rows)], axis=1
    ).astype(jnp.bfloat16)
    slot_parts = lax.dot_general(
        slot_match.astype(jnp.bfloat16),
        row_parts,
        (((0,), (0,)), ((), ())),
        preferred_element_type=jnp.float32,
    ).astype(jnp.int32)
    outgoing = jnp.where(
        slot_parts[:, 2] > 0, slot_parts[:, 0] * 32 + slot_parts[:, 1], -1
    )
    outgoing = outgoing.reshape(shards, capacity)
    incoming = lax.all_to_all(outgoing, "table", split_axis=0, concat_axis=0, tiled=True)
    flat_in = incoming.reshape(-1)
    row_match = (flat_in[:, None] == jnp.arange(rows_dev, dtype=jnp.int32)[None, :]).astype(
        jnp.bfloat16
    )
    fetched = jnp.dot(row_match, id_table, preferred_element_type=jnp.float32).astype(jnp.bfloat16)
    returned = lax.all_to_all(
        fetched.reshape(shards, capacity, emb_width), "table", split_axis=0, concat_axis=0, tiled=True
    )
    pair_targets = targets.reshape(batch * slots, bags)
    pool_match = pair_targets[:, 0:1] == slots_all[None, :]
    for bag in range(1, bags):
        pool_match = pool_match | (pair_targets[:, bag : bag + 1] == slots_all[None, :])
    pool_match = pool_match.astype(jnp.bfloat16)
    pooled = jnp.dot(
        pool_match,
        returned.reshape(shards * capacity, emb_width),
        preferred_element_type=jnp.float32,
    )
    pooled = pooled.astype(jnp.bfloat16).reshape(batch, slots, emb_width)
    query_in = pooled[:, :feats].reshape(batch, hidden_width)
    item_in = pooled[:, feats:].reshape(batch, hidden_width)
    query_vec = jnp.dot(query_in, query_tower, preferred_element_type=jnp.float32).astype(
        jnp.bfloat16
    )
    item_vec = jnp.dot(item_in, item_tower, preferred_element_type=jnp.float32).astype(jnp.bfloat16)
    n_dp = lax.axis_size("dp")
    dp_index = lax.axis_index("dp")
    table_index = lax.axis_index("table")
    both = jnp.concatenate([query_vec, item_vec], axis=1)
    both = lax.all_to_all(
        jnp.broadcast_to(both[None], (n_dp,) + both.shape), "dp", 0, 0, tiled=True
    )
    all_queries = both[:, :, :out_width].reshape(n_dp * batch, out_width)
    all_items = both[:, :, out_width:].reshape(n_dp * batch, out_width)
    scores = scale * lax.dot_general(
        all_queries, all_items, (((1,), (1,)), ((), ())), preferred_element_type=jnp.float32
    )
    peak = jnp.max(scores, axis=1, keepdims=True)
    log_total = peak + jnp.log(jnp.sum(jnp.exp(scores - peak), axis=1, keepdims=True))
    own = dp_index * batch
    row_scores = lax.dynamic_slice_in_dim(scores, own, batch, axis=0)
    row_total = lax.dynamic_slice_in_dim(log_total, own, batch, axis=0)
    col_scores = lax.dynamic_slice_in_dim(scores, own, batch, axis=1)
    row_probs = jnp.exp(row_scores - row_total).astype(jnp.bfloat16)
    col_probs = jnp.exp(col_scores - log_total).astype(jnp.bfloat16)
    query_grad = (
        scale
        * (
            jnp.dot(row_probs, all_items, preferred_element_type=jnp.float32)
            - item_vec.astype(jnp.float32)
        )
    ).astype(jnp.bfloat16)
    weighted = lax.dot_general(
        col_probs, all_queries, (((0,), (0,)), ((), ())), preferred_element_type=jnp.float32
    )
    item_grad = (scale * (weighted - query_vec.astype(jnp.float32))).astype(jnp.bfloat16)
    query_back = lax.dot_general(
        query_grad, query_tower, (((1,), (1,)), ((), ())), preferred_element_type=jnp.float32
    )
    item_back = lax.dot_general(
        item_grad, item_tower, (((1,), (1,)), ((), ())), preferred_element_type=jnp.float32
    )
    norm_sq = (
        squares(query_in) * squares(query_grad)
        + squares(item_in) * squares(item_grad)
        + squares(query_back)
        + squares(item_back)
    )
    factor = jnp.minimum(1.0, clip_norm / jnp.sqrt(norm_sq + 1e-06))
    clipped_query = (factor[:, None] * query_grad.astype(jnp.float32)).astype(jnp.bfloat16)
    clipped_item = (factor[:, None] * item_grad.astype(jnp.float32)).astype(jnp.bfloat16)
    tower_part = jnp.stack(
        [
            lax.dot_general(
                query_in,
                clipped_query,
                (((0,), (0,)), ((), ())),
                preferred_element_type=jnp.float32,
            ),
            lax.dot_general(
                item_in, clipped_item, (((0,), (0,)), ((), ())), preferred_element_type=jnp.float32
            ),
        ]
    )
    back_all = jnp.concatenate(
        [query_back.reshape(batch, feats, emb_width), item_back.reshape(batch, feats, emb_width)],
        axis=1,
    )
    lookup_grad = (factor[:, None, None] * back_all).astype(jnp.bfloat16)
    grad_out = lax.dot_general(
        pool_match,
        lookup_grad.reshape(batch * slots, emb_width),
        (((0,), (0,)), ((), ())),
        preferred_element_type=jnp.float32,
    ).astype(jnp.bfloat16)
    grad_in = lax.all_to_all(
        grad_out.reshape(shards, capacity, emb_width),
        "table",
        split_axis=0,
        concat_axis=0,
        tiled=True,
    )
    row_sum = lax.dot_general(
        row_match,
        grad_in.reshape(shards * capacity, emb_width),
        (((0,), (0,)), ((), ())),
        preferred_element_type=jnp.float32,
    )
    row_count = jnp.sum(row_match.astype(jnp.float32), axis=0)
    shard_rows = rows_dev // n_dp
    count_lanes = emb_width // shard_rows
    core = table_index % 2
    partner = [(i, i ^ 1) for i in range(shards)]
    kept = jnp.where(core == 0, tower_part[0], tower_part[1])
    sent = jnp.where(core == 0, tower_part[1], tower_part[0])
    chip_sum = kept + lax.ppermute(sent, "table", partner)
    dp_rows = hidden_width // n_dp
    chips = shards // 2
    own_rows = dp_rows // chips
    packed = jnp.concatenate(
        [
            chip_sum.reshape(n_dp, dp_rows, out_width),
            row_sum.reshape(n_dp, shard_rows, emb_width),
            jnp.broadcast_to(
                row_count.reshape(n_dp, 1, shard_rows, 1), (n_dp, 1, shard_rows, count_lanes)
            ).reshape(n_dp, 1, emb_width),
        ],
        axis=1,
    )
    packed = jnp.sum(lax.all_to_all(packed, "dp", 0, 0, tiled=True), axis=0)
    own_sum = packed[dp_rows : dp_rows + shard_rows]
    own_count = packed[dp_rows + shard_rows].reshape(shard_rows, count_lanes)[:, 0]
    own_seeds = lax.dynamic_slice_in_dim(row_seeds, dp_index * shard_rows, shard_rows)
    own_update = own_sum / clip_norm + NOISE_MULT * jnp.where(
        own_count[:, None] > 0.0, hashed_noise(own_seeds, emb_width), 0.0
    )
    chunks = packed[:dp_rows].reshape(chips, 1, own_rows, out_width)
    same_core = jnp.arange(2, dtype=jnp.int32)[None, :, None, None] == core
    part = jnp.where(same_core, chunks, 0.0).reshape(shards, own_rows, out_width)
    part = jnp.sum(lax.all_to_all(part, "table", 0, 0, tiled=True), axis=0)
    first_row = core * hidden_width + dp_index * dp_rows + (table_index // 2) * own_rows
    tower_seed_rows = lax.dynamic_slice_in_dim(
        tower_seeds.reshape(2 * hidden_width), first_row, own_rows
    )
    part = part / clip_norm + NOISE_MULT * hashed_noise(tower_seed_rows, out_width)
    part = lax.all_to_all(
        jnp.broadcast_to(part[None], (shards,) + part.shape), "table", 0, 0, tiled=True
    )
    part = part.reshape(chips, 2, own_rows, out_width)
    part = jnp.where(core == 0, part[:, 0], part[:, 1]).reshape(dp_rows, out_width)
    finished = jnp.concatenate([part, own_update], axis=0).astype(jnp.bfloat16)
    finished = lax.all_to_all(
        jnp.broadcast_to(finished[None], (n_dp,) + finished.shape), "dp", 0, 0, tiled=True
    )
    own_tower = finished[:, :dp_rows].reshape(hidden_width, out_width)
    other_tower = lax.ppermute(own_tower, "table", partner)
    tower_update = jnp.where(
        core == 0,
        jnp.stack([own_tower, other_tower]),
        jnp.stack([other_tower, own_tower]),
    ).astype(jnp.float32)
    table_update = finished[:, dp_rows:].reshape(rows_dev, emb_width).astype(jnp.float32)
    return (table_update, tower_update)


def solution(mesh):
    in_specs = (P("table", None), P(("dp", "table"), None, None), P(), P(), P(), P("table"), P())
    out_specs = (P("table", None), P())
    return jax.shard_map(body, mesh=mesh, in_specs=in_specs, out_specs=out_specs, check_vma=False)
```

```python
import math

import jax
import jax.numpy as jnp
from jax import lax
from jax.sharding import PartitionSpec as P

NOISE_MULT = 0.1


def hashed_noise(seed_rows, width):
    columns = jnp.arange(width, dtype=jnp.int32)
    summed = jnp.zeros(seed_rows.shape + (width,), jnp.float32)
    for section in range(2):
        mixed = seed_rows[..., None] + (columns * 2 + section) * 1013904223
        mixed = mixed ^ mixed >> 15 & 131071
        mixed = mixed * 73244475
        mixed = mixed ^ mixed >> 13 & 524287
        mixed = mixed * 1597334677
        mixed = mixed ^ mixed >> 16 & 65535
        lower = (mixed & 65535).astype(jnp.float32) / 65536.0 - 0.5
        upper = (mixed >> 16 & 65535).astype(jnp.float32) / 65536.0 - 0.5
        summed = summed + lower + upper
    return summed * math.sqrt(3.0)


def squares(values):
    return jnp.sum(jnp.square(values.astype(jnp.float32)), axis=1)


def body(id_table, lookup_ids, row_owner, query_tower, item_tower, row_seeds, tower_seeds):
    shards = lax.axis_size("table")
    rows_dev, emb_width = id_table.shape
    batch, slots, bags = lookup_ids.shape
    feats = slots // 2
    hidden_width, out_width = query_tower.shape
    scale = 200.0 / math.sqrt(out_width)
    clip_norm = 0.9 * math.sqrt(2.0 * hidden_width + 400.0)
    requests = batch * slots * bags
    capacity = 3 * requests // (2 * shards)
    flat_ids = lookup_ids.reshape(-1)
    lane_width = 128
    owner_blocks = row_owner.reshape(-1, lane_width)
    block_match = (
        (flat_ids // lane_width)[:, None]
        == jnp.arange(owner_blocks.shape[0], dtype=jnp.int32)[None, :]
    ).astype(jnp.bfloat16)
    owner_high = jnp.dot(
        block_match, (owner_blocks // 256).astype(jnp.bfloat16), preferred_element_type=jnp.float32
    )
    owner_low = jnp.dot(
        block_match, (owner_blocks % 256).astype(jnp.bfloat16), preferred_element_type=jnp.float32
    )
    lane_match = (flat_ids % lane_width)[:, None] == jnp.arange(lane_width, dtype=jnp.int32)[None, :]
    positions = jnp.sum(
        jnp.where(lane_match, owner_high.astype(jnp.int32) * 256 + owner_low.astype(jnp.int32), 0),
        axis=1,
    )
    owners = positions // rows_dev
    local_rows = positions - owners * rows_dev
    one_hot = owners[:, None] == jnp.arange(shards, dtype=jnp.int32)[None, :]
    order = jnp.arange(requests, dtype=jnp.int32)
    earlier = (order[None, :] < order[:, None]).astype(jnp.bfloat16)
    before = jnp.dot(earlier, one_hot.astype(jnp.bfloat16), preferred_element_type=jnp.float32)
    ranks = jnp.sum(jnp.where(one_hot, before, 0.0), axis=1).astype(jnp.int32)
    targets = owners * capacity + ranks
    slots_all = jnp.arange(shards * capacity, dtype=jnp.int32)
    slot_match = targets[:, None] == slots_all[None, :]
    row_parts = jnp.stack(
        [local_rows // 32, local_rows % 32, jnp.ones_like(local_rows)], axis=1
    ).astype(jnp.bfloat16)
    slot_parts = lax.dot_general(
        slot_match.astype(jnp.bfloat16),
        row_parts,
        (((0,), (0,)), ((), ())),
        preferred_element_type=jnp.float32,
    ).astype(jnp.int32)
    outgoing = jnp.where(
        slot_parts[:, 2] > 0, slot_parts[:, 0] * 32 + slot_parts[:, 1], -1
    )
    outgoing = outgoing.reshape(shards, capacity)
    incoming = lax.all_to_all(outgoing, "table", split_axis=0, concat_axis=0, tiled=True)
    flat_in = incoming.reshape(-1)
    row_match = (flat_in[:, None] == jnp.arange(rows_dev, dtype=jnp.int32)[None, :]).astype(
        jnp.bfloat16
    )
    fetched = jnp.dot(row_match, id_table, preferred_element_type=jnp.float32).astype(jnp.bfloat16)
    returned = lax.all_to_all(
        fetched.reshape(shards, capacity, emb_width), "table", split_axis=0, concat_axis=0, tiled=True
    )
    pair_targets = targets.reshape(batch * slots, bags)
    pool_match = pair_targets[:, 0:1] == slots_all[None, :]
    for bag in range(1, bags):
        pool_match = pool_match | (pair_targets[:, bag : bag + 1] == slots_all[None, :])
    pool_match = pool_match.astype(jnp.bfloat16)
    pooled = jnp.dot(
        pool_match,
        returned.reshape(shards * capacity, emb_width),
        preferred_element_type=jnp.float32,
    )
    pooled = pooled.astype(jnp.bfloat16).reshape(batch, slots, emb_width)
    query_in = pooled[:, :feats].reshape(batch, hidden_width)
    item_in = pooled[:, feats:].reshape(batch, hidden_width)
    query_vec = jnp.dot(query_in, query_tower, preferred_element_type=jnp.float32).astype(
        jnp.bfloat16
    )
    item_vec = jnp.dot(item_in, item_tower, preferred_element_type=jnp.float32).astype(jnp.bfloat16)
    n_dp = lax.axis_size("dp")
    dp_index = lax.axis_index("dp")
    table_index = lax.axis_index("table")
    both = jnp.concatenate([query_vec, item_vec], axis=1)
    both = lax.all_to_all(
        jnp.broadcast_to(both[None], (n_dp,) + both.shape), "dp", 0, 0, tiled=True
    )
    all_queries = both[:, :, :out_width].reshape(n_dp * batch, out_width)
    all_items = both[:, :, out_width:].reshape(n_dp * batch, out_width)
    contract = (((1,), (1,)), ((), ()))
    scores = scale * lax.dot_general(
        all_queries, all_items, contract, preferred_element_type=jnp.float32
    )
    peak = jnp.max(scores, axis=1, keepdims=True)
    again_queries, again_items = lax.optimization_barrier((all_queries, all_items))
    scores_again = scale * lax.dot_general(
        again_queries, again_items, contract, preferred_element_type=jnp.float32
    )
    log_total = peak + jnp.log(jnp.sum(jnp.exp(scores_again - peak), axis=1, keepdims=True))
    own = dp_index * batch
    own_queries = lax.dynamic_slice_in_dim(all_queries, own, batch, axis=0)
    own_items = lax.dynamic_slice_in_dim(all_items, own, batch, axis=0)
    row_scores = scale * lax.dot_general(
        own_queries, all_items, contract, preferred_element_type=jnp.float32
    )
    col_scores = scale * lax.dot_general(
        all_queries, own_items, contract, preferred_element_type=jnp.float32
    )
    row_total = lax.dynamic_slice_in_dim(log_total, own, batch, axis=0)
    row_probs = jnp.exp(row_scores - row_total).astype(jnp.bfloat16)
    col_probs = jnp.exp(col_scores - log_total).astype(jnp.bfloat16)
    query_grad = (
        scale
        * (
            jnp.dot(row_probs, all_items, preferred_element_type=jnp.float32)
            - item_vec.astype(jnp.float32)
        )
    ).astype(jnp.bfloat16)
    weighted = lax.dot_general(
        col_probs, all_queries, (((0,), (0,)), ((), ())), preferred_element_type=jnp.float32
    )
    item_grad = (scale * (weighted - query_vec.astype(jnp.float32))).astype(jnp.bfloat16)
    query_back = lax.dot_general(
        query_grad, query_tower, (((1,), (1,)), ((), ())), preferred_element_type=jnp.float32
    )
    item_back = lax.dot_general(
        item_grad, item_tower, (((1,), (1,)), ((), ())), preferred_element_type=jnp.float32
    )
    norm_sq = (
        squares(query_in) * squares(query_grad)
        + squares(item_in) * squares(item_grad)
        + squares(query_back)
        + squares(item_back)
    )
    factor = jnp.minimum(1.0, clip_norm / jnp.sqrt(norm_sq + 1e-06))
    clipped_query = (factor[:, None] * query_grad.astype(jnp.float32)).astype(jnp.bfloat16)
    clipped_item = (factor[:, None] * item_grad.astype(jnp.float32)).astype(jnp.bfloat16)
    tower_part = jnp.stack(
        [
            lax.dot_general(
                query_in,
                clipped_query,
                (((0,), (0,)), ((), ())),
                preferred_element_type=jnp.float32,
            ),
            lax.dot_general(
                item_in, clipped_item, (((0,), (0,)), ((), ())), preferred_element_type=jnp.float32
            ),
        ]
    )
    back_all = jnp.concatenate(
        [query_back.reshape(batch, feats, emb_width), item_back.reshape(batch, feats, emb_width)],
        axis=1,
    )
    lookup_grad = (factor[:, None, None] * back_all).astype(jnp.bfloat16)
    grad_out = lax.dot_general(
        pool_match,
        lookup_grad.reshape(batch * slots, emb_width),
        (((0,), (0,)), ((), ())),
        preferred_element_type=jnp.float32,
    ).astype(jnp.bfloat16)
    grad_in = lax.all_to_all(
        grad_out.reshape(shards, capacity, emb_width),
        "table",
        split_axis=0,
        concat_axis=0,
        tiled=True,
    )
    row_sum = lax.dot_general(
        row_match,
        grad_in.reshape(shards * capacity, emb_width),
        (((0,), (0,)), ((), ())),
        preferred_element_type=jnp.float32,
    )
    row_count = jnp.sum(row_match.astype(jnp.float32), axis=0)
    shard_rows = rows_dev // n_dp
    count_lanes = emb_width // shard_rows
    core = table_index % 2
    partner = [(i, i ^ 1) for i in range(shards)]
    kept = jnp.where(core == 0, tower_part[0], tower_part[1])
    sent = jnp.where(core == 0, tower_part[1], tower_part[0])
    chip_sum = kept + lax.ppermute(sent, "table", partner)
    dp_rows = hidden_width // n_dp
    chips = shards // 2
    own_rows = dp_rows // chips
    packed = jnp.concatenate(
        [
            chip_sum.reshape(n_dp, dp_rows, out_width),
            row_sum.reshape(n_dp, shard_rows, emb_width),
            jnp.broadcast_to(
                row_count.reshape(n_dp, 1, shard_rows, 1), (n_dp, 1, shard_rows, count_lanes)
            ).reshape(n_dp, 1, emb_width),
        ],
        axis=1,
    )
    packed = jnp.sum(lax.all_to_all(packed, "dp", 0, 0, tiled=True), axis=0)
    own_sum = packed[dp_rows : dp_rows + shard_rows]
    own_count = packed[dp_rows + shard_rows].reshape(shard_rows, count_lanes)[:, 0]
    own_seeds = lax.dynamic_slice_in_dim(row_seeds, dp_index * shard_rows, shard_rows)
    own_update = own_sum / clip_norm + NOISE_MULT * jnp.where(
        own_count[:, None] > 0.0, hashed_noise(own_seeds, emb_width), 0.0
    )
    chunks = packed[:dp_rows].reshape(chips, 1, own_rows, out_width)
    same_core = jnp.arange(2, dtype=jnp.int32)[None, :, None, None] == core
    part = jnp.where(same_core, chunks, 0.0).reshape(shards, own_rows, out_width)
    part = jnp.sum(lax.all_to_all(part, "table", 0, 0, tiled=True), axis=0)
    first_row = core * hidden_width + dp_index * dp_rows + (table_index // 2) * own_rows
    tower_seed_rows = lax.dynamic_slice_in_dim(
        tower_seeds.reshape(2 * hidden_width), first_row, own_rows
    )
    part = part / clip_norm + NOISE_MULT * hashed_noise(tower_seed_rows, out_width)
    part = lax.all_to_all(
        jnp.broadcast_to(part[None], (shards,) + part.shape), "table", 0, 0, tiled=True
    )
    part = part.reshape(chips, 2, own_rows, out_width)
    part = jnp.where(core == 0, part[:, 0], part[:, 1]).reshape(dp_rows, out_width)
    finished = jnp.concatenate([part, own_update], axis=0).astype(jnp.bfloat16)
    finished = lax.all_to_all(
        jnp.broadcast_to(finished[None], (n_dp,) + finished.shape), "dp", 0, 0, tiled=True
    )
    own_tower = finished[:, :dp_rows].reshape(hidden_width, out_width)
    other_tower = lax.ppermute(own_tower, "table", partner)
    tower_update = jnp.where(
        core == 0,
        jnp.stack([own_tower, other_tower]),
        jnp.stack([other_tower, own_tower]),
    ).astype(jnp.float32)
    table_update = finished[:, dp_rows:].reshape(rows_dev, emb_width).astype(jnp.float32)
    return (table_update, tower_update)


def solution(mesh):
    in_specs = (P("table", None), P(("dp", "table"), None, None), P(), P(), P(), P("table"), P())
    out_specs = (P("table", None), P())
    return jax.shard_map(body, mesh=mesh, in_specs=in_specs, out_specs=out_specs, check_vma=False)
```

```python
import math

import jax
import jax.numpy as jnp
from jax import lax
from jax.sharding import PartitionSpec as P

NOISE_MULT = 0.1


def hashed_noise(seed_rows, width):
    columns = jnp.arange(width, dtype=jnp.int32)
    summed = jnp.zeros(seed_rows.shape + (width,), jnp.float32)
    for section in range(2):
        mixed = seed_rows[..., None] + (columns * 2 + section) * 1013904223
        mixed = mixed ^ mixed >> 15 & 131071
        mixed = mixed * 73244475
        mixed = mixed ^ mixed >> 13 & 524287
        mixed = mixed * 1597334677
        mixed = mixed ^ mixed >> 16 & 65535
        lower = (mixed & 65535).astype(jnp.float32) / 65536.0 - 0.5
        upper = (mixed >> 16 & 65535).astype(jnp.float32) / 65536.0 - 0.5
        summed = summed + lower + upper
    return summed * math.sqrt(3.0)


def squares(values):
    return jnp.sum(jnp.square(values.astype(jnp.float32)), axis=1)


def body(id_table, lookup_ids, row_owner, query_tower, item_tower, row_seeds, tower_seeds):
    shards = lax.axis_size("table")
    rows_dev, emb_width = id_table.shape
    batch, slots, bags = lookup_ids.shape
    feats = slots // 2
    hidden_width, out_width = query_tower.shape
    scale = 200.0 / math.sqrt(out_width)
    clip_norm = 0.9 * math.sqrt(2.0 * hidden_width + 400.0)
    requests = batch * slots * bags
    capacity = 3 * requests // (2 * shards)
    flat_ids = lookup_ids.reshape(-1)
    lane_width = 128
    owner_blocks = row_owner.reshape(-1, lane_width)
    block_match = (
        (flat_ids // lane_width)[:, None]
        == jnp.arange(owner_blocks.shape[0], dtype=jnp.int32)[None, :]
    ).astype(jnp.bfloat16)
    owner_high = jnp.dot(
        block_match, (owner_blocks // 256).astype(jnp.bfloat16), preferred_element_type=jnp.float32
    )
    owner_low = jnp.dot(
        block_match, (owner_blocks % 256).astype(jnp.bfloat16), preferred_element_type=jnp.float32
    )
    lane_match = (flat_ids % lane_width)[:, None] == jnp.arange(lane_width, dtype=jnp.int32)[None, :]
    positions = jnp.sum(
        jnp.where(lane_match, owner_high.astype(jnp.int32) * 256 + owner_low.astype(jnp.int32), 0),
        axis=1,
    )
    owners = positions // rows_dev
    local_rows = positions - owners * rows_dev
    one_hot = owners[:, None] == jnp.arange(shards, dtype=jnp.int32)[None, :]
    order = jnp.arange(requests, dtype=jnp.int32)
    earlier = (order[None, :] < order[:, None]).astype(jnp.bfloat16)
    before = jnp.dot(earlier, one_hot.astype(jnp.bfloat16), preferred_element_type=jnp.float32)
    ranks = jnp.sum(jnp.where(one_hot, before, 0.0), axis=1).astype(jnp.int32)
    targets = owners * capacity + ranks
    slots_all = jnp.arange(shards * capacity, dtype=jnp.int32)
    slot_match = targets[:, None] == slots_all[None, :]
    row_parts = jnp.stack(
        [local_rows // 32, local_rows % 32, jnp.ones_like(local_rows)], axis=1
    ).astype(jnp.bfloat16)
    slot_parts = lax.dot_general(
        slot_match.astype(jnp.bfloat16),
        row_parts,
        (((0,), (0,)), ((), ())),
        preferred_element_type=jnp.float32,
    ).astype(jnp.int32)
    outgoing = jnp.where(
        slot_parts[:, 2] > 0, slot_parts[:, 0] * 32 + slot_parts[:, 1], -1
    )
    outgoing = outgoing.reshape(shards, capacity)
    incoming = lax.all_to_all(outgoing, "table", split_axis=0, concat_axis=0, tiled=True)
    flat_in = incoming.reshape(-1)
    row_match = (flat_in[:, None] == jnp.arange(rows_dev, dtype=jnp.int32)[None, :]).astype(
        jnp.bfloat16
    )
    fetched = jnp.dot(row_match, id_table, preferred_element_type=jnp.float32).astype(jnp.bfloat16)
    returned = lax.all_to_all(
        fetched.reshape(shards, capacity, emb_width), "table", split_axis=0, concat_axis=0, tiled=True
    )
    pair_targets = targets.reshape(batch * slots, bags)
    pool_match = pair_targets[:, 0:1] == slots_all[None, :]
    for bag in range(1, bags):
        pool_match = pool_match | (pair_targets[:, bag : bag + 1] == slots_all[None, :])
    pool_match = pool_match.astype(jnp.bfloat16)
    pooled = jnp.dot(
        pool_match,
        returned.reshape(shards * capacity, emb_width),
        preferred_element_type=jnp.float32,
    )
    pooled = pooled.astype(jnp.bfloat16).reshape(batch, slots, emb_width)
    query_in = pooled[:, :feats].reshape(batch, hidden_width)
    item_in = pooled[:, feats:].reshape(batch, hidden_width)
    query_vec = jnp.dot(query_in, query_tower, preferred_element_type=jnp.float32).astype(
        jnp.bfloat16
    )
    item_vec = jnp.dot(item_in, item_tower, preferred_element_type=jnp.float32).astype(jnp.bfloat16)
    n_dp = lax.axis_size("dp")
    dp_index = lax.axis_index("dp")
    table_index = lax.axis_index("table")
    both = jnp.concatenate([query_vec, item_vec], axis=1)
    both = lax.all_to_all(
        jnp.broadcast_to(both[None], (n_dp,) + both.shape), "dp", 0, 0, tiled=True
    )
    all_queries = both[:, :, :out_width].reshape(n_dp * batch, out_width)
    all_items = both[:, :, out_width:].reshape(n_dp * batch, out_width)
    contract = (((1,), (1,)), ((), ()))
    scores = scale * lax.dot_general(
        all_queries, all_items, contract, preferred_element_type=jnp.float32
    )
    peak = jnp.max(scores, axis=1, keepdims=True)
    again_queries, again_items = lax.optimization_barrier((all_queries, all_items))
    scores_again = scale * lax.dot_general(
        again_queries, again_items, contract, preferred_element_type=jnp.float32
    )
    log_total = peak + jnp.log(jnp.sum(jnp.exp(scores_again - peak), axis=1, keepdims=True))
    own = dp_index * batch
    own_queries = lax.dynamic_slice_in_dim(all_queries, own, batch, axis=0)
    own_items = lax.dynamic_slice_in_dim(all_items, own, batch, axis=0)
    row_scores = scale * lax.dot_general(
        own_queries, all_items, contract, preferred_element_type=jnp.float32
    )
    col_scores = scale * lax.dot_general(
        all_queries, own_items, contract, preferred_element_type=jnp.float32
    )
    row_total = lax.dynamic_slice_in_dim(log_total, own, batch, axis=0)
    row_probs = jnp.exp(row_scores - row_total).astype(jnp.bfloat16)
    col_probs = jnp.exp(col_scores - log_total).astype(jnp.bfloat16)
    query_grad = (
        scale
        * (
            jnp.dot(row_probs, all_items, preferred_element_type=jnp.float32)
            - item_vec.astype(jnp.float32)
        )
    ).astype(jnp.bfloat16)
    weighted = lax.dot_general(
        col_probs, all_queries, (((0,), (0,)), ((), ())), preferred_element_type=jnp.float32
    )
    item_grad = (scale * (weighted - query_vec.astype(jnp.float32))).astype(jnp.bfloat16)
    query_back = lax.dot_general(
        query_grad, query_tower, (((1,), (1,)), ((), ())), preferred_element_type=jnp.float32
    )
    item_back = lax.dot_general(
        item_grad, item_tower, (((1,), (1,)), ((), ())), preferred_element_type=jnp.float32
    )
    norm_sq = (
        squares(query_in) * squares(query_grad)
        + squares(item_in) * squares(item_grad)
        + squares(query_back)
        + squares(item_back)
    )
    factor = jnp.minimum(1.0, clip_norm / jnp.sqrt(norm_sq + 1e-06))
    clipped_query = (factor[:, None] * query_grad.astype(jnp.float32)).astype(jnp.bfloat16)
    clipped_item = (factor[:, None] * item_grad.astype(jnp.float32)).astype(jnp.bfloat16)
    tower_part = jnp.stack(
        [
            lax.dot_general(
                query_in,
                clipped_query,
                (((0,), (0,)), ((), ())),
                preferred_element_type=jnp.float32,
            ),
            lax.dot_general(
                item_in, clipped_item, (((0,), (0,)), ((), ())), preferred_element_type=jnp.float32
            ),
        ]
    )
    back_all = jnp.concatenate(
        [query_back.reshape(batch, feats, emb_width), item_back.reshape(batch, feats, emb_width)],
        axis=1,
    )
    lookup_grad = (factor[:, None, None] * back_all).astype(jnp.bfloat16)
    pool_match_t = slots_all[:, None] == pair_targets[None, :, 0]
    for bag in range(1, bags):
        pool_match_t = pool_match_t | (slots_all[:, None] == pair_targets[None, :, bag])
    grad_out = jnp.dot(
        pool_match_t.astype(jnp.bfloat16),
        lookup_grad.reshape(batch * slots, emb_width),
        preferred_element_type=jnp.float32,
    ).astype(jnp.bfloat16)
    grad_in = lax.all_to_all(
        grad_out.reshape(shards, capacity, emb_width),
        "table",
        split_axis=0,
        concat_axis=0,
        tiled=True,
    )
    row_match_t = (jnp.arange(rows_dev, dtype=jnp.int32)[:, None] == flat_in[None, :]).astype(
        jnp.bfloat16
    )
    row_sum = jnp.dot(
        row_match_t,
        grad_in.reshape(shards * capacity, emb_width),
        preferred_element_type=jnp.float32,
    )
    row_count = jnp.sum(row_match.astype(jnp.float32), axis=0)
    shard_rows = rows_dev // n_dp
    count_lanes = emb_width // shard_rows
    core = table_index % 2
    partner = [(i, i ^ 1) for i in range(shards)]
    kept = jnp.where(core == 0, tower_part[0], tower_part[1])
    sent = jnp.where(core == 0, tower_part[1], tower_part[0])
    chip_sum = kept + lax.ppermute(sent, "table", partner)
    dp_rows = hidden_width // n_dp
    chips = shards // 2
    own_rows = dp_rows // chips
    packed = jnp.concatenate(
        [
            chip_sum.reshape(n_dp, dp_rows, out_width),
            row_sum.reshape(n_dp, shard_rows, emb_width),
            jnp.broadcast_to(
                row_count.reshape(n_dp, 1, shard_rows, 1), (n_dp, 1, shard_rows, count_lanes)
            ).reshape(n_dp, 1, emb_width),
        ],
        axis=1,
    )
    packed = jnp.sum(lax.all_to_all(packed, "dp", 0, 0, tiled=True), axis=0)
    own_sum = packed[dp_rows : dp_rows + shard_rows]
    own_count = packed[dp_rows + shard_rows].reshape(shard_rows, count_lanes)[:, 0]
    own_seeds = lax.dynamic_slice_in_dim(row_seeds, dp_index * shard_rows, shard_rows)
    own_update = own_sum / clip_norm + NOISE_MULT * jnp.where(
        own_count[:, None] > 0.0, hashed_noise(own_seeds, emb_width), 0.0
    )
    chunks = packed[:dp_rows].reshape(chips, 1, own_rows, out_width)
    same_core = jnp.arange(2, dtype=jnp.int32)[None, :, None, None] == core
    part = jnp.where(same_core, chunks, 0.0).reshape(shards, own_rows, out_width)
    part = jnp.sum(lax.all_to_all(part, "table", 0, 0, tiled=True), axis=0)
    first_row = core * hidden_width + dp_index * dp_rows + (table_index // 2) * own_rows
    tower_seed_rows = lax.dynamic_slice_in_dim(
        tower_seeds.reshape(2 * hidden_width), first_row, own_rows
    )
    part = part / clip_norm + NOISE_MULT * hashed_noise(tower_seed_rows, out_width)
    part = lax.all_to_all(
        jnp.broadcast_to(part[None], (shards,) + part.shape), "table", 0, 0, tiled=True
    )
    part = part.reshape(chips, 2, own_rows, out_width)
    part = jnp.where(core == 0, part[:, 0], part[:, 1]).reshape(dp_rows, out_width)
    finished = jnp.concatenate([part, own_update], axis=0).astype(jnp.bfloat16)
    finished = lax.all_to_all(
        jnp.broadcast_to(finished[None], (n_dp,) + finished.shape), "dp", 0, 0, tiled=True
    )
    own_tower = finished[:, :dp_rows].reshape(hidden_width, out_width)
    other_tower = lax.ppermute(own_tower, "table", partner)
    tower_update = jnp.where(
        core == 0,
        jnp.stack([own_tower, other_tower]),
        jnp.stack([other_tower, own_tower]),
    ).astype(jnp.float32)
    table_update = finished[:, dp_rows:].reshape(rows_dev, emb_width).astype(jnp.float32)
    return (table_update, tower_update)


def solution(mesh):
    in_specs = (P("table", None), P(("dp", "table"), None, None), P(), P(), P(), P("table"), P())
    out_specs = (P("table", None), P())
    return jax.shard_map(body, mesh=mesh, in_specs=in_specs, out_specs=out_specs, check_vma=False)
```

```python
import math

import jax
import jax.numpy as jnp
from jax import lax
from jax.sharding import PartitionSpec as P

NOISE_MULT = 0.1


def hashed_noise(seed_rows, width):
    columns = jnp.arange(width, dtype=jnp.int32)
    summed = jnp.zeros(seed_rows.shape + (width,), jnp.float32)
    for section in range(2):
        mixed = seed_rows[..., None] + (columns * 2 + section) * 1013904223
        mixed = mixed ^ mixed >> 15 & 131071
        mixed = mixed * 73244475
        mixed = mixed ^ mixed >> 13 & 524287
        mixed = mixed * 1597334677
        mixed = mixed ^ mixed >> 16 & 65535
        lower = (mixed & 65535).astype(jnp.float32) / 65536.0 - 0.5
        upper = (mixed >> 16 & 65535).astype(jnp.float32) / 65536.0 - 0.5
        summed = summed + lower + upper
    return summed * math.sqrt(3.0)


def squares(values):
    return jnp.sum(jnp.square(values.astype(jnp.float32)), axis=1)


def body(id_table, lookup_ids, row_owner, query_tower, item_tower, row_seeds, tower_seeds):
    shards = lax.axis_size("table")
    rows_dev, emb_width = id_table.shape
    batch, slots, bags = lookup_ids.shape
    feats = slots // 2
    hidden_width, out_width = query_tower.shape
    scale = 200.0 / math.sqrt(out_width)
    clip_norm = 0.9 * math.sqrt(2.0 * hidden_width + 400.0)
    requests = batch * slots * bags
    capacity = 3 * requests // (2 * shards)
    flat_ids = lookup_ids.reshape(-1)
    lane_width = 128
    owner_blocks = row_owner.reshape(-1, lane_width)
    block_match = (
        (flat_ids // lane_width)[:, None]
        == jnp.arange(owner_blocks.shape[0], dtype=jnp.int32)[None, :]
    ).astype(jnp.bfloat16)
    owner_high = jnp.dot(
        block_match, (owner_blocks // 256).astype(jnp.bfloat16), preferred_element_type=jnp.float32
    )
    owner_low = jnp.dot(
        block_match, (owner_blocks % 256).astype(jnp.bfloat16), preferred_element_type=jnp.float32
    )
    lane_match = (flat_ids % lane_width)[:, None] == jnp.arange(lane_width, dtype=jnp.int32)[None, :]
    positions = jnp.sum(
        jnp.where(lane_match, owner_high.astype(jnp.int32) * 256 + owner_low.astype(jnp.int32), 0),
        axis=1,
    )
    owners = positions // rows_dev
    local_rows = positions - owners * rows_dev
    one_hot = owners[:, None] == jnp.arange(shards, dtype=jnp.int32)[None, :]
    order = jnp.arange(requests, dtype=jnp.int32)
    earlier = (order[None, :] < order[:, None]).astype(jnp.bfloat16)
    before = jnp.dot(earlier, one_hot.astype(jnp.bfloat16), preferred_element_type=jnp.float32)
    ranks = jnp.sum(jnp.where(one_hot, before, 0.0), axis=1).astype(jnp.int32)
    targets = owners * capacity + ranks
    slots_all = jnp.arange(shards * capacity, dtype=jnp.int32)
    slot_match = targets[:, None] == slots_all[None, :]
    row_parts = jnp.stack(
        [local_rows // 32, local_rows % 32, jnp.ones_like(local_rows)], axis=0
    ).astype(jnp.bfloat16)
    slot_parts = jnp.dot(
        row_parts, slot_match.astype(jnp.bfloat16), preferred_element_type=jnp.float32
    ).astype(jnp.int32)
    outgoing = jnp.where(slot_parts[2] > 0, slot_parts[0] * 32 + slot_parts[1], -1)
    outgoing = outgoing.reshape(shards, capacity)
    incoming = lax.all_to_all(outgoing, "table", split_axis=0, concat_axis=0, tiled=True)
    flat_in = incoming.reshape(-1)
    row_match = (flat_in[:, None] == jnp.arange(rows_dev, dtype=jnp.int32)[None, :]).astype(
        jnp.bfloat16
    )
    fetched = jnp.dot(row_match, id_table, preferred_element_type=jnp.float32).astype(jnp.bfloat16)
    returned = lax.all_to_all(
        fetched.reshape(shards, capacity, emb_width), "table", split_axis=0, concat_axis=0, tiled=True
    )
    pair_targets = targets.reshape(batch * slots, bags)
    pool_match = pair_targets[:, 0:1] == slots_all[None, :]
    for bag in range(1, bags):
        pool_match = pool_match | (pair_targets[:, bag : bag + 1] == slots_all[None, :])
    pool_match = pool_match.astype(jnp.bfloat16)
    pooled = jnp.dot(
        pool_match,
        returned.reshape(shards * capacity, emb_width),
        preferred_element_type=jnp.float32,
    )
    pooled = pooled.astype(jnp.bfloat16).reshape(batch, slots, emb_width)
    query_in = pooled[:, :feats].reshape(batch, hidden_width)
    item_in = pooled[:, feats:].reshape(batch, hidden_width)
    query_vec = jnp.dot(query_in, query_tower, preferred_element_type=jnp.float32).astype(
        jnp.bfloat16
    )
    item_vec = jnp.dot(item_in, item_tower, preferred_element_type=jnp.float32).astype(jnp.bfloat16)
    n_dp = lax.axis_size("dp")
    dp_index = lax.axis_index("dp")
    table_index = lax.axis_index("table")
    both = jnp.concatenate([query_vec, item_vec], axis=1)
    both = lax.all_to_all(
        jnp.broadcast_to(both[None], (n_dp,) + both.shape), "dp", 0, 0, tiled=True
    )
    all_queries = both[:, :, :out_width].reshape(n_dp * batch, out_width)
    all_items = both[:, :, out_width:].reshape(n_dp * batch, out_width)
    contract = (((1,), (1,)), ((), ()))
    scores = scale * lax.dot_general(
        all_queries, all_items, contract, preferred_element_type=jnp.float32
    )
    peak = jnp.max(scores, axis=1, keepdims=True)
    again_queries, again_items = lax.optimization_barrier((all_queries, all_items))
    scores_again = scale * lax.dot_general(
        again_queries, again_items, contract, preferred_element_type=jnp.float32
    )
    log_total = peak + jnp.log(jnp.sum(jnp.exp(scores_again - peak), axis=1, keepdims=True))
    own = dp_index * batch
    own_queries = lax.dynamic_slice_in_dim(all_queries, own, batch, axis=0)
    own_items = lax.dynamic_slice_in_dim(all_items, own, batch, axis=0)
    row_scores = scale * lax.dot_general(
        own_queries, all_items, contract, preferred_element_type=jnp.float32
    )
    col_scores = scale * lax.dot_general(
        all_queries, own_items, contract, preferred_element_type=jnp.float32
    )
    row_total = lax.dynamic_slice_in_dim(log_total, own, batch, axis=0)
    row_probs = jnp.exp(row_scores - row_total).astype(jnp.bfloat16)
    col_probs = jnp.exp(col_scores - log_total).astype(jnp.bfloat16)
    query_grad = (
        scale
        * (
            jnp.dot(row_probs, all_items, preferred_element_type=jnp.float32)
            - item_vec.astype(jnp.float32)
        )
    ).astype(jnp.bfloat16)
    weighted = lax.dot_general(
        col_probs, all_queries, (((0,), (0,)), ((), ())), preferred_element_type=jnp.float32
    )
    item_grad = (scale * (weighted - query_vec.astype(jnp.float32))).astype(jnp.bfloat16)
    query_back = lax.dot_general(
        query_grad, query_tower, (((1,), (1,)), ((), ())), preferred_element_type=jnp.float32
    )
    item_back = lax.dot_general(
        item_grad, item_tower, (((1,), (1,)), ((), ())), preferred_element_type=jnp.float32
    )
    norm_sq = (
        squares(query_in) * squares(query_grad)
        + squares(item_in) * squares(item_grad)
        + squares(query_back)
        + squares(item_back)
    )
    factor = jnp.minimum(1.0, clip_norm / jnp.sqrt(norm_sq + 1e-06))
    clipped_query = (factor[:, None] * query_grad.astype(jnp.float32)).astype(jnp.bfloat16)
    clipped_item = (factor[:, None] * item_grad.astype(jnp.float32)).astype(jnp.bfloat16)
    tower_part = jnp.stack(
        [
            lax.dot_general(
                query_in,
                clipped_query,
                (((0,), (0,)), ((), ())),
                preferred_element_type=jnp.float32,
            ),
            lax.dot_general(
                item_in, clipped_item, (((0,), (0,)), ((), ())), preferred_element_type=jnp.float32
            ),
        ]
    )
    back_all = jnp.concatenate(
        [query_back.reshape(batch, feats, emb_width), item_back.reshape(batch, feats, emb_width)],
        axis=1,
    )
    lookup_grad = (factor[:, None, None] * back_all).astype(jnp.bfloat16)
    pool_match_t = slots_all[:, None] == pair_targets[None, :, 0]
    for bag in range(1, bags):
        pool_match_t = pool_match_t | (slots_all[:, None] == pair_targets[None, :, bag])
    grad_out = jnp.dot(
        pool_match_t.astype(jnp.bfloat16),
        lookup_grad.reshape(batch * slots, emb_width),
        preferred_element_type=jnp.float32,
    ).astype(jnp.bfloat16)
    grad_in = lax.all_to_all(
        grad_out.reshape(shards, capacity, emb_width),
        "table",
        split_axis=0,
        concat_axis=0,
        tiled=True,
    )
    row_match_t = (jnp.arange(rows_dev, dtype=jnp.int32)[:, None] == flat_in[None, :]).astype(
        jnp.bfloat16
    )
    row_sum = jnp.dot(
        row_match_t,
        grad_in.reshape(shards * capacity, emb_width),
        preferred_element_type=jnp.float32,
    )
    row_count = jnp.sum(row_match.astype(jnp.float32), axis=0)
    shard_rows = rows_dev // n_dp
    count_lanes = emb_width // shard_rows
    core = table_index % 2
    partner = [(i, i ^ 1) for i in range(shards)]
    kept = jnp.where(core == 0, tower_part[0], tower_part[1])
    sent = jnp.where(core == 0, tower_part[1], tower_part[0])
    chip_sum = kept + lax.ppermute(sent, "table", partner)
    dp_rows = hidden_width // n_dp
    chips = shards // 2
    own_rows = dp_rows // chips
    packed = jnp.concatenate(
        [
            chip_sum.reshape(n_dp, dp_rows, out_width),
            row_sum.reshape(n_dp, shard_rows, emb_width),
            jnp.broadcast_to(
                row_count.reshape(n_dp, 1, shard_rows, 1), (n_dp, 1, shard_rows, count_lanes)
            ).reshape(n_dp, 1, emb_width),
        ],
        axis=1,
    )
    packed = jnp.sum(lax.all_to_all(packed, "dp", 0, 0, tiled=True), axis=0)
    own_sum = packed[dp_rows : dp_rows + shard_rows]
    own_count = packed[dp_rows + shard_rows].reshape(shard_rows, count_lanes)[:, 0]
    own_seeds = lax.dynamic_slice_in_dim(row_seeds, dp_index * shard_rows, shard_rows)
    own_update = own_sum / clip_norm + NOISE_MULT * jnp.where(
        own_count[:, None] > 0.0, hashed_noise(own_seeds, emb_width), 0.0
    )
    chunks = packed[:dp_rows].reshape(chips, 1, own_rows, out_width)
    same_core = jnp.arange(2, dtype=jnp.int32)[None, :, None, None] == core
    part = jnp.where(same_core, chunks, 0.0).reshape(shards, own_rows, out_width)
    part = jnp.sum(lax.all_to_all(part, "table", 0, 0, tiled=True), axis=0)
    first_row = core * hidden_width + dp_index * dp_rows + (table_index // 2) * own_rows
    tower_seed_rows = lax.dynamic_slice_in_dim(
        tower_seeds.reshape(2 * hidden_width), first_row, own_rows
    )
    part = part / clip_norm + NOISE_MULT * hashed_noise(tower_seed_rows, out_width)
    part = lax.all_to_all(
        jnp.broadcast_to(part[None], (shards,) + part.shape), "table", 0, 0, tiled=True
    )
    part = part.reshape(chips, 2, own_rows, out_width)
    part = jnp.where(core == 0, part[:, 0], part[:, 1]).reshape(dp_rows, out_width)
    finished = jnp.concatenate([part, own_update], axis=0).astype(jnp.bfloat16)
    finished = lax.all_to_all(
        jnp.broadcast_to(finished[None], (n_dp,) + finished.shape), "dp", 0, 0, tiled=True
    )
    own_tower = finished[:, :dp_rows].reshape(hidden_width, out_width)
    other_tower = lax.ppermute(own_tower, "table", partner)
    tower_update = jnp.where(
        core == 0,
        jnp.stack([own_tower, other_tower]),
        jnp.stack([other_tower, own_tower]),
    ).astype(jnp.float32)
    table_update = finished[:, dp_rows:].reshape(rows_dev, emb_width).astype(jnp.float32)
    return (table_update, tower_update)


def solution(mesh):
    in_specs = (P("table", None), P(("dp", "table"), None, None), P(), P(), P(), P("table"), P())
    out_specs = (P("table", None), P())
    return jax.shard_map(body, mesh=mesh, in_specs=in_specs, out_specs=out_specs, check_vma=False)
```

```python
import math

import jax
import jax.numpy as jnp
from jax import lax
from jax.sharding import PartitionSpec as P

NOISE_MULT = 0.1


def hashed_noise(seed_rows, width):
    columns = jnp.arange(width, dtype=jnp.int32)
    summed = jnp.zeros(seed_rows.shape + (width,), jnp.float32)
    for section in range(2):
        mixed = seed_rows[..., None] + (columns * 2 + section) * 1013904223
        mixed = mixed ^ mixed >> 15 & 131071
        mixed = mixed * 73244475
        mixed = mixed ^ mixed >> 13 & 524287
        mixed = mixed * 1597334677
        mixed = mixed ^ mixed >> 16 & 65535
        lower = (mixed & 65535).astype(jnp.float32) / 65536.0 - 0.5
        upper = (mixed >> 16 & 65535).astype(jnp.float32) / 65536.0 - 0.5
        summed = summed + lower + upper
    return summed * math.sqrt(3.0)


def squares(values):
    return jnp.sum(jnp.square(values.astype(jnp.float32)), axis=1)


def body(id_table, lookup_ids, row_owner, query_tower, item_tower, row_seeds, tower_seeds):
    shards = lax.axis_size("table")
    rows_dev, emb_width = id_table.shape
    batch, slots, bags = lookup_ids.shape
    feats = slots // 2
    hidden_width, out_width = query_tower.shape
    scale = 200.0 / math.sqrt(out_width)
    clip_norm = 0.9 * math.sqrt(2.0 * hidden_width + 400.0)
    requests = batch * slots * bags
    capacity = 3 * requests // (2 * shards)
    flat_ids = lookup_ids.reshape(-1)
    lane_width = 128
    owner_blocks = row_owner.reshape(-1, lane_width)
    block_match = (
        (flat_ids // lane_width)[:, None]
        == jnp.arange(owner_blocks.shape[0], dtype=jnp.int32)[None, :]
    ).astype(jnp.bfloat16)
    owner_high = jnp.dot(
        block_match, (owner_blocks // 256).astype(jnp.bfloat16), preferred_element_type=jnp.float32
    )
    owner_low = jnp.dot(
        block_match, (owner_blocks % 256).astype(jnp.bfloat16), preferred_element_type=jnp.float32
    )
    lane_match = (flat_ids % lane_width)[:, None] == jnp.arange(lane_width, dtype=jnp.int32)[None, :]
    positions = jnp.sum(
        jnp.where(lane_match, owner_high.astype(jnp.int32) * 256 + owner_low.astype(jnp.int32), 0),
        axis=1,
    )
    owners = positions // rows_dev
    local_rows = positions - owners * rows_dev
    one_hot = owners[:, None] == jnp.arange(shards, dtype=jnp.int32)[None, :]
    order = jnp.arange(requests, dtype=jnp.int32)
    earlier = (order[None, :] < order[:, None]).astype(jnp.bfloat16)
    before = jnp.dot(earlier, one_hot.astype(jnp.bfloat16), preferred_element_type=jnp.float32)
    ranks = jnp.sum(jnp.where(one_hot, before, 0.0), axis=1).astype(jnp.int32)
    targets = owners * capacity + ranks
    slots_all = jnp.arange(shards * capacity, dtype=jnp.int32)
    slot_match = targets[:, None] == slots_all[None, :]
    row_parts = jnp.stack(
        [local_rows // 32, local_rows % 32, jnp.ones_like(local_rows)], axis=0
    ).astype(jnp.bfloat16)
    slot_parts = jnp.dot(
        row_parts, slot_match.astype(jnp.bfloat16), preferred_element_type=jnp.float32
    ).astype(jnp.int32)
    outgoing = jnp.where(slot_parts[2] > 0, slot_parts[0] * 32 + slot_parts[1], -1)
    outgoing = outgoing.reshape(shards, capacity)
    incoming = lax.all_to_all(outgoing, "table", split_axis=0, concat_axis=0, tiled=True)
    flat_in = incoming.reshape(-1)
    row_match = (flat_in[:, None] == jnp.arange(rows_dev, dtype=jnp.int32)[None, :]).astype(
        jnp.bfloat16
    )
    fetched = jnp.dot(row_match, id_table, preferred_element_type=jnp.float32).astype(jnp.bfloat16)
    returned = lax.all_to_all(
        fetched.reshape(shards, capacity, emb_width), "table", split_axis=0, concat_axis=0, tiled=True
    )
    pair_targets = targets.reshape(batch * slots, bags)
    pool_match = pair_targets[:, 0:1] == slots_all[None, :]
    for bag in range(1, bags):
        pool_match = pool_match | (pair_targets[:, bag : bag + 1] == slots_all[None, :])
    pool_match = pool_match.astype(jnp.bfloat16)
    pooled = jnp.dot(
        pool_match,
        returned.reshape(shards * capacity, emb_width),
        preferred_element_type=jnp.float32,
    )
    pooled = pooled.astype(jnp.bfloat16).reshape(batch, slots, emb_width)
    query_in = pooled[:, :feats].reshape(batch, hidden_width)
    item_in = pooled[:, feats:].reshape(batch, hidden_width)
    query_vec = jnp.dot(query_in, query_tower, preferred_element_type=jnp.float32).astype(
        jnp.bfloat16
    )
    item_vec = jnp.dot(item_in, item_tower, preferred_element_type=jnp.float32).astype(jnp.bfloat16)
    n_dp = lax.axis_size("dp")
    dp_index = lax.axis_index("dp")
    table_index = lax.axis_index("table")
    both = jnp.concatenate([query_vec, item_vec], axis=1)
    both = lax.all_to_all(
        jnp.broadcast_to(both[None], (n_dp,) + both.shape), "dp", 0, 0, tiled=True
    )
    all_queries = both[:, :, :out_width].reshape(n_dp * batch, out_width)
    all_items = both[:, :, out_width:].reshape(n_dp * batch, out_width)
    contract = (((1,), (1,)), ((), ()))
    scores = scale * lax.dot_general(
        all_queries, all_items, contract, preferred_element_type=jnp.float32
    )
    peak = jnp.max(scores, axis=1, keepdims=True)
    again_queries, again_items = lax.optimization_barrier((all_queries, all_items))
    scores_again = scale * lax.dot_general(
        again_queries, again_items, contract, preferred_element_type=jnp.float32
    )
    log_total = peak + jnp.log(jnp.sum(jnp.exp(scores_again - peak), axis=1, keepdims=True))
    own = dp_index * batch
    own_queries = lax.dynamic_slice_in_dim(all_queries, own, batch, axis=0)
    own_items = lax.dynamic_slice_in_dim(all_items, own, batch, axis=0)
    row_scores = scale * lax.dot_general(
        own_queries, all_items, contract, preferred_element_type=jnp.float32
    )
    col_scores = scale * lax.dot_general(
        all_queries, own_items, contract, preferred_element_type=jnp.float32
    )
    row_total = lax.dynamic_slice_in_dim(log_total, own, batch, axis=0)
    row_probs = jnp.exp(row_scores - row_total).astype(jnp.bfloat16)
    col_probs = jnp.exp(col_scores - log_total).astype(jnp.bfloat16)
    query_grad = (
        scale
        * (
            jnp.dot(row_probs, all_items, preferred_element_type=jnp.float32)
            - item_vec.astype(jnp.float32)
        )
    ).astype(jnp.bfloat16)
    weighted = lax.dot_general(
        col_probs, all_queries, (((0,), (0,)), ((), ())), preferred_element_type=jnp.float32
    )
    item_grad = (scale * (weighted - query_vec.astype(jnp.float32))).astype(jnp.bfloat16)
    query_back = lax.dot_general(
        query_grad, query_tower, (((1,), (1,)), ((), ())), preferred_element_type=jnp.float32
    )
    item_back = lax.dot_general(
        item_grad, item_tower, (((1,), (1,)), ((), ())), preferred_element_type=jnp.float32
    )
    norm_sq = (
        squares(query_in) * squares(query_grad)
        + squares(item_in) * squares(item_grad)
        + squares(query_back)
        + squares(item_back)
    )
    factor = jnp.minimum(1.0, clip_norm / jnp.sqrt(norm_sq + 1e-06))
    clipped_query = (factor[:, None] * query_grad.astype(jnp.float32)).astype(jnp.bfloat16)
    clipped_item = (factor[:, None] * item_grad.astype(jnp.float32)).astype(jnp.bfloat16)
    tower_part = jnp.stack(
        [
            lax.dot_general(
                query_in,
                clipped_query,
                (((0,), (0,)), ((), ())),
                preferred_element_type=jnp.float32,
            ),
            lax.dot_general(
                item_in, clipped_item, (((0,), (0,)), ((), ())), preferred_element_type=jnp.float32
            ),
        ]
    )
    back_all = jnp.concatenate(
        [query_back.reshape(batch, feats, emb_width), item_back.reshape(batch, feats, emb_width)],
        axis=1,
    )
    lookup_grad = (factor[:, None, None] * back_all).astype(jnp.bfloat16)
    pool_match_t = slots_all[:, None] == pair_targets[None, :, 0]
    for bag in range(1, bags):
        pool_match_t = pool_match_t | (slots_all[:, None] == pair_targets[None, :, bag])
    grad_out = jnp.dot(
        pool_match_t.astype(jnp.bfloat16),
        lookup_grad.reshape(batch * slots, emb_width),
        preferred_element_type=jnp.float32,
    ).astype(jnp.bfloat16)
    grad_in = lax.all_to_all(
        grad_out.reshape(shards, capacity, emb_width),
        "table",
        split_axis=0,
        concat_axis=0,
        tiled=True,
    )
    row_match_t = (jnp.arange(rows_dev, dtype=jnp.int32)[:, None] == flat_in[None, :]).astype(
        jnp.bfloat16
    )
    row_sum = jnp.dot(
        row_match_t,
        grad_in.reshape(shards * capacity, emb_width),
        preferred_element_type=jnp.float32,
    )
    row_count = jnp.sum(row_match.astype(jnp.float32), axis=0)
    shard_rows = rows_dev // n_dp
    count_lanes = emb_width // shard_rows
    core = table_index % 2
    partner = [(i, i ^ 1) for i in range(shards)]
    kept = jnp.where(core == 0, tower_part[0], tower_part[1])
    sent = jnp.where(core == 0, tower_part[1], tower_part[0])
    chip_sum = kept + lax.ppermute(sent, "table", partner)
    dp_rows = hidden_width // n_dp
    chips = shards // 2
    own_rows = dp_rows // chips
    packed = jnp.concatenate(
        [
            chip_sum.reshape(n_dp, dp_rows, out_width),
            row_sum.reshape(n_dp, shard_rows, emb_width),
            jnp.broadcast_to(
                row_count.reshape(n_dp, 1, shard_rows, 1), (n_dp, 1, shard_rows, count_lanes)
            ).reshape(n_dp, 1, emb_width),
        ],
        axis=1,
    )
    packed = jnp.sum(lax.all_to_all(packed, "dp", 0, 0, tiled=True), axis=0)
    own_sum = packed[dp_rows : dp_rows + shard_rows]
    own_count = packed[dp_rows + shard_rows].reshape(shard_rows, count_lanes)[:, 0]
    own_seeds = lax.dynamic_slice_in_dim(row_seeds, dp_index * shard_rows, shard_rows)
    own_update = own_sum / clip_norm + NOISE_MULT * jnp.where(
        own_count[:, None] > 0.0, hashed_noise(own_seeds, emb_width), 0.0
    )
    chunks = packed[:dp_rows].reshape(chips, 1, own_rows, out_width)
    same_core = jnp.arange(2, dtype=jnp.int32)[None, :, None, None] == core
    part = jnp.where(same_core, chunks, 0.0).reshape(shards, own_rows, out_width)
    part = jnp.sum(lax.all_to_all(part, "table", 0, 0, tiled=True), axis=0)
    first_row = core * hidden_width + dp_index * dp_rows + (table_index // 2) * own_rows
    tower_seed_rows = lax.dynamic_slice_in_dim(
        tower_seeds.reshape(2 * hidden_width), first_row, own_rows
    )
    part = part / clip_norm + NOISE_MULT * hashed_noise(tower_seed_rows, out_width)
    part = lax.all_to_all(
        jnp.broadcast_to(part[None], (shards,) + part.shape), "table", 0, 0, tiled=True
    )
    part = part.reshape(chips, 2, own_rows, out_width)
    part = jnp.where(core == 0, part[:, 0], part[:, 1]).reshape(dp_rows, out_width)
    finished = jnp.concatenate([part, own_update], axis=0).astype(jnp.bfloat16)
    finished = lax.all_to_all(
        jnp.broadcast_to(finished[None], (n_dp,) + finished.shape), "dp", 0, 0, tiled=True
    )
    own_tower = finished[:, :dp_rows].reshape(hidden_width, out_width)
    other_tower = lax.ppermute(own_tower, "table", partner)
    tower_update = lax.dynamic_slice_in_dim(
        jnp.stack([own_tower, other_tower, own_tower]), core, 2, axis=0
    ).astype(jnp.float32)
    table_update = finished[:, dp_rows:].reshape(rows_dev, emb_width).astype(jnp.float32)
    return (table_update, tower_update)


def solution(mesh):
    in_specs = (P("table", None), P(("dp", "table"), None, None), P(), P(), P(), P("table"), P())
    out_specs = (P("table", None), P())
    return jax.shard_map(body, mesh=mesh, in_specs=in_specs, out_specs=out_specs, check_vma=False)
```
